512 devices in a mesh: frame: 32 (over x, z_lo), row: 16 (over y, z_hi, core).
Axes of the slice: x: 4, y: 4, z: 16 (z_hi: 2, z_lo: 8; z = z_hi * 8 + z_lo), core: 2. Of those that a mesh axis runs over, the one named last changes fastest.
Arguments:
- tokens: bfloat16 [32, 4096, 512], P('frame', 'row'), may hold values from -15 to 15
- norm_spatial: float32 [512], replicated, may hold values from 0.25 to 1.75
- w_spatial: bfloat16 [512, 1536], replicated, may hold values from -10 to 10
- w_spatial_out: bfloat16 [512, 512], replicated, may hold values from -0.25 to 0.25
- norm_temporal: float32 [512], replicated, may hold values from 0.25 to 1.75
- w_temporal: bfloat16 [512, 1536], replicated, may hold values from -10 to 10
- w_temporal_out: bfloat16 [512, 512], replicated, may hold values from -0.25 to 0.25
Outputs:
- mixed: bfloat16 [32, 4096, 512], P('frame', 'row')
The draws below stay inside these ranges and needn't reach their ends.
All inputs are finite; a program needn't handle non-finite values.
Results may differ from the reference program's by a relative error of at most 0.01.
The reference program's roundings to bfloat16 on the way count: a program that leaves them out, or rounds other values in their place, can miss the bound.
Values may be sent and summed in bfloat16 or wider, within the bound.
No kernel may reach another device: no remote copies, remote signals or barrier semaphores. Data moves between devices by JAX's collectives and lax.ppermute only.
A program may use at most 64 MiB of HBM per device.

```python
import math
import jax
import jax.numpy as jnp
from jax import lax

D = 512
HEADS = 8
HEAD = 64
CELLS = 4096
FRAMES = 32


def attention_weights(key):
    root = 1.0 / math.sqrt(D)
    query = jnp.clip(jax.random.normal(jax.random.fold_in(key, 1), (D, D), jnp.float32), -6.0, 6.0) * (1.6 * root)
    keys = jnp.clip(jax.random.normal(jax.random.fold_in(key, 2), (D, D), jnp.float32), -6.0, 6.0) * (1.6 * root)
    values = jnp.clip(jax.random.normal(jax.random.fold_in(key, 3), (D, D), jnp.float32), -6.0, 6.0) * root
    return jnp.concatenate([query, keys, values], axis=1).astype(jnp.bfloat16)


def draw_w_spatial(key, part):
    return attention_weights(jax.random.fold_in(key, 101))


def draw_w_temporal(key, part):
    return attention_weights(jax.random.fold_in(key, 202))


def draw_tokens(key, part):
    base = jnp.clip(jax.random.normal(jax.random.fold_in(key, 11), (FRAMES, CELLS, D), jnp.float32), -6.0, 6.0)
    return base.astype(jnp.bfloat16)


def normal_values(own_key, shape, width, limit, kind=jnp.bfloat16):
    array = width * jax.random.normal(own_key, shape, jnp.float32)
    return jnp.clip(array, min=-limit, max=limit).astype(kind)


def setup_inputs(seed: int = 0) -> dict:
    splits = jax.random.split(jax.random.key(seed), 8)
    return {
        "tokens": draw_tokens(jax.random.fold_in(splits[7], 71), 0),
        "norm_spatial": jnp.clip(1.0 + 0.15 * jax.random.normal(splits[1], (D,), jnp.float32), 0.25, 1.75),
        "w_spatial": draw_w_spatial(jax.random.fold_in(splits[7], 71), 0),
        "w_spatial_out": normal_values(splits[3], (D, D), D ** -0.5, 0.25),
        "norm_temporal": jnp.clip(1.0 + 0.15 * jax.random.normal(splits[4], (D,), jnp.float32), 0.25, 1.75),
        "w_temporal": draw_w_temporal(jax.random.fold_in(splits[7], 71), 0),
        "w_temporal_out": normal_values(splits[6], (D, D), D ** -0.5, 0.25),
    }


def layer_norm(rows, gain):
    mean = lax.optimization_barrier(jnp.mean(rows, axis=-1, keepdims=True))
    centred = rows - mean
    spread = lax.optimization_barrier(jnp.mean(centred * centred, axis=-1, keepdims=True))
    return centred * lax.rsqrt(spread + 1e-05) * gain

def spatial_frame(qkv_frame):
    scale = 1.0 / HEAD ** 0.5

    def one_head(head):
        start = head * HEAD
        query = lax.dynamic_slice_in_dim(qkv_frame, start, HEAD, 1)
        keys = lax.dynamic_slice_in_dim(qkv_frame, D + start, HEAD, 1)
        values = lax.dynamic_slice_in_dim(qkv_frame, 2 * D + start, HEAD, 1)
        scores = jnp.dot(query, keys.T, preferred_element_type=jnp.float32) * scale
        peak = lax.optimization_barrier(jnp.max(scores, axis=1, keepdims=True))
        weights = jnp.exp(scores - peak)
        total = lax.optimization_barrier(jnp.sum(weights, axis=1, keepdims=True))
        return jnp.dot(weights.astype(jnp.bfloat16), values, preferred_element_type=jnp.float32) / total
    heads_out = lax.map(one_head, jnp.arange(HEADS, dtype=jnp.int32))
    return jnp.transpose(heads_out, (1, 0, 2)).reshape(CELLS, D).astype(jnp.bfloat16)

def temporal_cells(qkv):
    frames, cells = (qkv.shape[0], qkv.shape[1])
    scale = 1.0 / HEAD ** 0.5
    query = qkv[:, :, :D].astype(jnp.float32).reshape(frames, cells, HEADS, HEAD)
    keys = qkv[:, :, D:2 * D].astype(jnp.float32).reshape(frames, cells, HEADS, HEAD)
    values = qkv[:, :, 2 * D:].astype(jnp.float32).reshape(frames, cells, HEADS, HEAD)
    scores = jnp.einsum('fche,gche->chfg', query, keys) * scale
    later = jnp.arange(frames)[:, None] >= jnp.arange(frames)[None, :]
    scores = jnp.where(later, scores, -1e+30)
    peak = lax.optimization_barrier(jnp.max(scores, axis=3, keepdims=True))
    weights = jnp.exp(scores - peak)
    total = lax.optimization_barrier(jnp.sum(weights, axis=3))
    rounded = lax.optimization_barrier(weights.astype(jnp.bfloat16)).astype(jnp.float32)
    summed = jnp.einsum('chfg,gche->fche', rounded, values)
    context = summed / jnp.transpose(total, (2, 0, 1))[..., None]
    return context.reshape(frames, cells, D).astype(jnp.bfloat16)

def reference(tokens, norm_spatial, w_spatial, w_spatial_out, norm_temporal, w_temporal, w_temporal_out):
    resid = tokens.astype(jnp.float32)
    normed = layer_norm(resid, norm_spatial).astype(jnp.bfloat16)

    def frame_step(rows):
        qkv = jnp.dot(rows, w_spatial, preferred_element_type=jnp.float32).astype(jnp.bfloat16)
        return spatial_frame(qkv)
    context = lax.map(frame_step, normed)
    spatial = jnp.dot(context.reshape(FRAMES * CELLS, D), w_spatial_out, preferred_element_type=jnp.float32)
    after = resid + spatial.reshape(FRAMES, CELLS, D)
    second = layer_norm(after, norm_temporal).astype(jnp.bfloat16)
    qkv_t = jnp.dot(second.reshape(FRAMES * CELLS, D), w_temporal, preferred_element_type=jnp.float32)
    qkv_t = qkv_t.astype(jnp.bfloat16).reshape(FRAMES, CELLS, 3 * D)
    context_t = temporal_cells(qkv_t)
    temporal = jnp.dot(context_t.reshape(FRAMES * CELLS, D), w_temporal_out, preferred_element_type=jnp.float32)
    return (after + temporal.reshape(FRAMES, CELLS, D)).astype(jnp.bfloat16)
```

```python
import math

import jax
import jax.numpy as jnp
from jax import lax
from jax.experimental import pallas as pl
from jax.experimental.pallas import tpu as pltpu
from jax.sharding import Mesh
from jax.sharding import PartitionSpec as P

HEADS = 8
PAIR = 2


def layer_norm(rows, gain):
    mean = jnp.mean(rows, axis=-1, keepdims=True)
    centred = rows - mean
    spread = jnp.mean(centred * centred, axis=-1, keepdims=True)
    return centred * lax.rsqrt(spread + 1e-05) * gain


def spatial_kernel(q_ref, k_ref, v_ref, o_ref, *, size, scale):
    for h in range(PAIR):
        cols = slice(h * size, (h + 1) * size)
        query = q_ref[:, cols]
        keys = k_ref[:, cols]
        values = v_ref[:, cols]
        scores = (
            lax.dot_general(
                query, keys, (((1,), (1,)), ((), ())), preferred_element_type=jnp.float32
            )
            * scale
        )
        peak = jnp.max(scores, axis=1, keepdims=True)
        weights = jnp.exp(scores - peak)
        total = jnp.sum(weights, axis=1, keepdims=True)
        summed = jnp.dot(
            weights.astype(jnp.bfloat16), values, preferred_element_type=jnp.float32
        )
        o_ref[:, cols] = (summed / total).astype(o_ref.dtype)


def spatial_attention(query, keys, values):
    count, width = query.shape
    length = keys.shape[0]
    size = width // HEADS
    block = PAIR * size
    kernel = lambda *refs: spatial_kernel(*refs, size=size, scale=1.0 / math.sqrt(size))
    return pl.pallas_call(
        kernel,
        grid=(width // block,),
        in_specs=[
            pl.BlockSpec((count, block), lambda h: (0, h)),
            pl.BlockSpec((length, block), lambda h: (0, h)),
            pl.BlockSpec((length, block), lambda h: (0, h)),
        ],
        out_specs=pl.BlockSpec((count, block), lambda h: (0, h)),
        out_shape=jax.ShapeDtypeStruct((count, width), jnp.bfloat16),
        compiler_params=pltpu.CompilerParams(vmem_limit_bytes=48 * 1024 * 1024),
    )(query, keys, values)


def attend_cells(block_qkv):
    frames, cells = (block_qkv.shape[0], block_qkv.shape[1])
    width = block_qkv.shape[2] // 3
    size = width // HEADS
    scale = 1.0 / math.sqrt(size)
    query = block_qkv[:, :, :width].reshape(frames, cells, HEADS, size)
    keys = block_qkv[:, :, width : 2 * width].reshape(frames, cells, HEADS, size)
    values = block_qkv[:, :, 2 * width :].reshape(frames, cells, HEADS, size)
    scores = jnp.einsum("fche,gche->chfg", query, keys, preferred_element_type=jnp.float32) * scale
    later = jnp.arange(frames)[:, None] >= jnp.arange(frames)[None, :]
    scores = jnp.where(later, scores, -1e30)
    peak = jnp.max(scores, axis=3, keepdims=True)
    weights = jnp.exp(scores - peak)
    total = jnp.sum(weights, axis=3)
    summed = jnp.einsum(
        "chfg,gche->fche", weights.astype(jnp.bfloat16), values, preferred_element_type=jnp.float32
    )
    context = summed / jnp.transpose(total, (2, 0, 1))[..., None]
    return context.reshape(frames, cells, width).astype(jnp.bfloat16)


def shards(
    tokens, norm_spatial, w_spatial, w_spatial_out, norm_temporal, w_temporal, w_temporal_out
):
    frames_here, rows, width = tokens.shape
    count = frames_here * rows
    resid = tokens.reshape(count, width).astype(jnp.float32)
    normed = layer_norm(resid, norm_spatial).astype(jnp.bfloat16)
    query = jnp.dot(normed, w_spatial[:, :width], preferred_element_type=jnp.float32).astype(
        jnp.bfloat16
    )
    piece = lax.all_gather(normed, "core", axis=0, tiled=True)
    piece = lax.all_gather(piece, "zhi", axis=0, tiled=True)
    piece = lax.all_gather(piece, "y", axis=0, tiled=True)
    pairs = jnp.dot(piece, w_spatial[:, width:], preferred_element_type=jnp.float32).astype(
        jnp.bfloat16
    )
    context = spatial_attention(query, pairs[:, :width], pairs[:, width:])
    after = resid + jnp.dot(context, w_spatial_out, preferred_element_type=jnp.float32)
    second = layer_norm(after, norm_temporal).astype(jnp.bfloat16)
    owners = lax.axis_size(("x", "zlo"))
    share = rows // owners
    second = second.reshape(frames_here, owners, share, width)
    gathered = lax.all_to_all(second, ("x", "zlo"), split_axis=1, concat_axis=0, tiled=True)
    frames_all = gathered.shape[0]
    qkv_t = jnp.dot(
        gathered.reshape(frames_all * share, width), w_temporal, preferred_element_type=jnp.float32
    ).astype(jnp.bfloat16)
    context_t = attend_cells(qkv_t.reshape(frames_all, share, 3 * width))
    context_t = context_t.reshape(frames_all, 1, share, width)
    returned = lax.all_to_all(context_t, ("x", "zlo"), split_axis=0, concat_axis=1, tiled=True)
    mixed = after + jnp.dot(
        returned.reshape(count, width), w_temporal_out, preferred_element_type=jnp.float32
    )
    return mixed.reshape(frames_here, rows, width).astype(jnp.bfloat16)


def solution(mesh):
    frame_n, row_n = mesh.devices.shape
    devices = mesh.devices.reshape(4, frame_n // 4, row_n // 4, 2, 2)
    fine = Mesh(devices, ("x", "zlo", "y", "zhi", "core"))
    grid_spec = P(("x", "zlo"), ("y", "zhi", "core"), None)
    in_specs = (grid_spec, P(), P(), P(), P(), P(), P())
    return jax.shard_map(shards, mesh=fine, in_specs=in_specs, out_specs=grid_spec, check_vma=False)
```

```python
import math

import jax
import jax.numpy as jnp
from jax import lax
from jax.experimental import pallas as pl
from jax.experimental.pallas import tpu as pltpu
from jax.sharding import Mesh

from jax.sharding import PartitionSpec as P

HEADS = 8
PAIR = 2


def layer_norm(rows, gain):
    mean = jnp.mean(rows, axis=-1, keepdims=True)
    centred = rows - mean
    spread = jnp.mean(centred * centred, axis=-1, keepdims=True)
    return centred * lax.rsqrt(spread + 1e-05) * gain


def _head_scores(q_ref, k_ref, cols, scale):
    return (
        lax.dot_general(
            q_ref[:, cols], k_ref[:, cols], (((1,), (1,)), ((), ())),
            preferred_element_type=jnp.float32,
        )
        * scale
    )


def partial_kernel(q_ref, k_ref, v_ref, o_ref, m_ref, l_ref, *, size, scale):
    count = q_ref.shape[0]
    for h in range(PAIR):
        cols = slice(h * size, (h + 1) * size)
        scores = _head_scores(q_ref, k_ref, cols, scale)
        peak = jnp.max(scores, axis=1, keepdims=True)
        weights = jnp.exp(scores - peak)
        total = jnp.sum(weights, axis=1, keepdims=True)
        o_ref[:, cols] = jnp.dot(
            weights.astype(jnp.bfloat16), v_ref[:, cols], preferred_element_type=jnp.float32
        )
        m_ref[:, cols] = jnp.broadcast_to(peak, (count, size))
        l_ref[:, cols] = jnp.broadcast_to(total, (count, size))


def final_kernel(q_ref, k_ref, v_ref, o1_ref, m1_ref, l1_ref, out_ref, *, size, scale):
    for h in range(PAIR):
        cols = slice(h * size, (h + 1) * size)
        first = slice(h * size, h * size + 1)
        scores = _head_scores(q_ref, k_ref, cols, scale)
        before = m1_ref[:, first]
        peak = jnp.maximum(before, jnp.max(scores, axis=1, keepdims=True))
        weights = jnp.exp(scores - peak)
        fade = jnp.exp(before - peak)
        total = l1_ref[:, first] * fade + jnp.sum(weights, axis=1, keepdims=True)
        summed = o1_ref[:, cols] * fade + jnp.dot(
            weights.astype(jnp.bfloat16), v_ref[:, cols], preferred_element_type=jnp.float32
        )
        out_ref[:, cols] = (summed / total).astype(out_ref.dtype)


def _attention_call(kernel, query, keys, values, state, outs):
    count, width = query.shape
    length = keys.shape[0]
    size = width // HEADS
    block = PAIR * size
    body = lambda *refs: kernel(*refs, size=size, scale=1.0 / math.sqrt(size))
    row_block = pl.BlockSpec((count, block), lambda h: (0, h))
    key_block = pl.BlockSpec((length, block), lambda h: (0, h))
    return pl.pallas_call(
        body,
        grid=(width // block,),
        in_specs=[row_block, key_block, key_block] + [row_block] * len(state),
        out_specs=[row_block] * len(outs),
        out_shape=[jax.ShapeDtypeStruct((count, width), dtype) for dtype in outs],
        compiler_params=pltpu.CompilerParams(vmem_limit_bytes=48 * 1024 * 1024),
    )(query, keys, values, *state)


def spatial_partial(query, keys, values):
    return _attention_call(partial_kernel, query, keys, values, (), (jnp.float32,) * 3)


def spatial_final(query, keys, values, state):
    return _attention_call(final_kernel, query, keys, values, state, (jnp.bfloat16,))[0]


def spread_y(rows):
    rows = lax.all_gather(rows, "core", axis=0, tiled=True)
    ring = lax.axis_size("y")
    pieces = [rows]
    for shift in range(1, ring):
        pairs = [(i, (i + shift) % ring) for i in range(ring)]
        pieces.append(lax.ppermute(rows, "y", pairs))
    return jnp.concatenate(pieces, axis=0)


def attend_cells(block_qkv):
    frames, cells = (block_qkv.shape[0], block_qkv.shape[1])
    width = block_qkv.shape[2] // 3
    size = width // HEADS
    scale = 1.0 / math.sqrt(size)
    query = block_qkv[:, :, :width].reshape(frames, cells, HEADS, size)
    keys = block_qkv[:, :, width : 2 * width].reshape(frames, cells, HEADS, size)
    values = block_qkv[:, :, 2 * width :].reshape(frames, cells, HEADS, size)
    scores = jnp.einsum("fche,gche->chfg", query, keys, preferred_element_type=jnp.float32) * scale
    later = jnp.arange(frames)[:, None] >= jnp.arange(frames)[None, :]
    scores = jnp.where(later, scores, -1e30)
    peak = jnp.max(scores, axis=3, keepdims=True)
    weights = jnp.exp(scores - peak)
    total = jnp.sum(weights, axis=3)
    summed = jnp.einsum(
        "chfg,gche->fche", weights.astype(jnp.bfloat16), values, preferred_element_type=jnp.float32
    )
    context = summed / jnp.transpose(total, (2, 0, 1))[..., None]
    return context.reshape(frames, cells, width).astype(jnp.bfloat16)


def layer(
    tokens, norm_spatial, w_spatial, w_spatial_out, norm_temporal, w_temporal, w_temporal_out
):
    frames_here, rows, width = tokens.shape
    count = frames_here * rows
    resid = tokens.reshape(count, width).astype(jnp.float32)
    normed = layer_norm(resid, norm_spatial).astype(jnp.bfloat16)
    query = jnp.dot(normed, w_spatial[:, :width], preferred_element_type=jnp.float32).astype(
        jnp.bfloat16
    )
    partner = lax.ppermute(normed, "zhi", [(0, 1), (1, 0)])
    w_pairs = w_spatial[:, width:]
    near_rows = spread_y(normed)
    near = jnp.dot(near_rows, w_pairs, preferred_element_type=jnp.float32).astype(jnp.bfloat16)
    state = spatial_partial(query, near[:, :width], near[:, width:])
    far = jnp.dot(spread_y(partner), w_pairs, preferred_element_type=jnp.float32).astype(
        jnp.bfloat16
    )
    context = spatial_final(query, far[:, :width], far[:, width:], state)
    after = resid + jnp.dot(context, w_spatial_out, preferred_element_type=jnp.float32)
    second = layer_norm(after, norm_temporal).astype(jnp.bfloat16)
    owners = lax.axis_size(("x", "zlo"))
    share = rows // owners
    second = second.reshape(frames_here, owners, share, width)
    gathered = lax.all_to_all(second, ("x", "zlo"), split_axis=1, concat_axis=0, tiled=True)
    frames_all = gathered.shape[0]
    qkv_t = jnp.dot(
        gathered.reshape(frames_all * share, width), w_temporal, preferred_element_type=jnp.float32
    ).astype(jnp.bfloat16)
    context_t = attend_cells(qkv_t.reshape(frames_all, share, 3 * width))
    context_t = context_t.reshape(frames_all, 1, share, width)
    returned = lax.all_to_all(context_t, ("x", "zlo"), split_axis=0, concat_axis=1, tiled=True)
    mixed = after + jnp.dot(
        returned.reshape(count, width), w_temporal_out, preferred_element_type=jnp.float32
    )
    return mixed.reshape(frames_here, rows, width).astype(jnp.bfloat16)


def solution(mesh):
    frame_n, row_n = mesh.devices.shape
    devices = mesh.devices.reshape(4, frame_n // 4, row_n // 4, 2, 2)
    fine = Mesh(devices, ("x", "zlo", "y", "zhi", "core"))
    grid_spec = P(("x", "zlo"), ("y", "zhi", "core"), None)
    in_specs = (grid_spec, P(), P(), P(), P(), P(), P())
    return jax.shard_map(layer, mesh=fine, in_specs=in_specs, out_specs=grid_spec, check_vma=False)
```

```python
import math

import jax
import jax.numpy as jnp
from jax import lax
from jax.experimental import pallas as pl
from jax.experimental.pallas import tpu as pltpu
from jax.sharding import Mesh

from jax.sharding import PartitionSpec as P

HEADS = 8
PAIR = 2


def layer_norm(rows, gain):
    mean = jnp.mean(rows, axis=-1, keepdims=True)
    centred = rows - mean
    spread = jnp.mean(centred * centred, axis=-1, keepdims=True)
    return centred * lax.rsqrt(spread + 1e-05) * gain


def _head_scores(q_ref, k_ref, cols, scale):
    return (
        lax.dot_general(
            q_ref[:, cols], k_ref[:, cols], (((1,), (1,)), ((), ())),
            preferred_element_type=jnp.float32,
        )
        * scale
    )


def partial_kernel(q_ref, k_ref, v_ref, o_ref, m_ref, l_ref, *, size, scale):
    count = q_ref.shape[0]
    for h in range(PAIR):
        cols = slice(h * size, (h + 1) * size)
        scores = _head_scores(q_ref, k_ref, cols, scale)
        peak = jnp.max(scores, axis=1, keepdims=True)
        weights = jnp.exp(scores - peak)
        total = jnp.sum(weights, axis=1, keepdims=True)
        o_ref[:, cols] = jnp.dot(
            weights.astype(jnp.bfloat16), v_ref[:, cols], preferred_element_type=jnp.float32
        )
        m_ref[:, cols] = jnp.broadcast_to(peak, (count, size))
        l_ref[:, cols] = jnp.broadcast_to(total, (count, size))


def final_kernel(q_ref, k_ref, v_ref, o1_ref, m1_ref, l1_ref, out_ref, *, size, scale):
    for h in range(PAIR):
        cols = slice(h * size, (h + 1) * size)
        first = slice(h * size, h * size + 1)
        scores = _head_scores(q_ref, k_ref, cols, scale)
        before = m1_ref[:, first]
        peak = jnp.maximum(before, jnp.max(scores, axis=1, keepdims=True))
        weights = jnp.exp(scores - peak)
        fade = jnp.exp(before - peak)
        total = l1_ref[:, first] * fade + jnp.sum(weights, axis=1, keepdims=True)
        summed = o1_ref[:, cols] * fade + jnp.dot(
            weights.astype(jnp.bfloat16), v_ref[:, cols], preferred_element_type=jnp.float32
        )
        out_ref[:, cols] = (summed / total).astype(out_ref.dtype)


def _attention_call(kernel, query, keys, values, state, outs):
    count, width = query.shape
    length = keys.shape[0]
    size = width // HEADS
    block = PAIR * size
    body = lambda *refs: kernel(*refs, size=size, scale=1.0 / math.sqrt(size))
    row_block = pl.BlockSpec((count, block), lambda h: (0, h))
    key_block = pl.BlockSpec((length, block), lambda h: (0, h))
    return pl.pallas_call(
        body,
        grid=(width // block,),
        in_specs=[row_block, key_block, key_block] + [row_block] * len(state),
        out_specs=[row_block] * len(outs),
        out_shape=[jax.ShapeDtypeStruct((count, width), dtype) for dtype in outs],
        compiler_params=pltpu.CompilerParams(vmem_limit_bytes=48 * 1024 * 1024),
    )(query, keys, values, *state)


def spatial_partial(query, keys, values):
    return _attention_call(partial_kernel, query, keys, values, (), (jnp.float32,) * 3)


def spatial_final(query, keys, values, state):
    return _attention_call(final_kernel, query, keys, values, state, (jnp.bfloat16,))[0]


def spread_y(rows):
    rows = lax.all_gather(rows, "core", axis=0, tiled=True)
    ring = lax.axis_size("y")
    pieces = [rows]
    for shift in range(1, ring):
        pairs = [(i, (i + shift) % ring) for i in range(ring)]
        pieces.append(lax.ppermute(rows, "y", pairs))
    return jnp.concatenate(pieces, axis=0)


def attend_cells(block_qkv):
    frames, cells = (block_qkv.shape[0], block_qkv.shape[1])
    width = block_qkv.shape[2] // 3
    size = width // HEADS
    scale = 1.0 / math.sqrt(size)
    query = block_qkv[:, :, :width].reshape(frames, cells, HEADS, size)
    keys = block_qkv[:, :, width : 2 * width].reshape(frames, cells, HEADS, size)
    values = block_qkv[:, :, 2 * width :].reshape(frames, cells, HEADS, size)
    scores = jnp.einsum("fche,gche->chfg", query, keys, preferred_element_type=jnp.float32) * scale
    later = jnp.arange(frames)[:, None] >= jnp.arange(frames)[None, :]
    scores = jnp.where(later, scores, -1e30)
    peak = jnp.max(scores, axis=3, keepdims=True)
    weights = jnp.exp(scores - peak)
    total = jnp.sum(weights, axis=3)
    summed = jnp.einsum(
        "chfg,gche->fche", weights.astype(jnp.bfloat16), values, preferred_element_type=jnp.float32
    )
    context = summed / jnp.transpose(total, (2, 0, 1))[..., None]
    return context.reshape(frames, cells, width).astype(jnp.bfloat16)


def layer(
    tokens, norm_spatial, w_spatial, w_spatial_out, norm_temporal, w_temporal, w_temporal_out
):
    frames_here, rows, width = tokens.shape
    count = frames_here * rows
    resid = tokens.reshape(count, width).astype(jnp.float32)
    normed = layer_norm(resid, norm_spatial).astype(jnp.bfloat16)
    query = jnp.dot(normed, w_spatial[:, :width], preferred_element_type=jnp.float32).astype(
        jnp.bfloat16
    )
    partner = lax.ppermute(normed, "zhi", [(0, 1), (1, 0)])
    w_pairs = w_spatial[:, width:]
    near_rows = spread_y(normed)
    near = jnp.dot(near_rows, w_pairs, preferred_element_type=jnp.float32).astype(jnp.bfloat16)
    state = spatial_partial(query, near[:, :width], near[:, width:])
    far_rows = spread_y(partner)
    far = jnp.dot(far_rows, w_pairs, preferred_element_type=jnp.float32).astype(jnp.bfloat16)
    context = spatial_final(query, far[:, :width], far[:, width:], state)
    after = resid + jnp.dot(context, w_spatial_out, preferred_element_type=jnp.float32)
    second = layer_norm(after, norm_temporal).astype(jnp.bfloat16)
    owners = lax.axis_size(("x", "zlo"))
    share = rows // owners
    second = second.reshape(frames_here, owners, share, width)
    gathered = lax.all_to_all(second, ("x", "zlo"), split_axis=1, concat_axis=0, tiled=True)
    frames_all = gathered.shape[0]
    qkv_t = jnp.dot(
        gathered.reshape(frames_all * share, width), w_temporal, preferred_element_type=jnp.float32
    ).astype(jnp.bfloat16)
    context_t = attend_cells(qkv_t.reshape(frames_all, share, 3 * width))
    context_t = context_t.reshape(frames_all, 1, share, width)
    returned = lax.all_to_all(context_t, ("x", "zlo"), split_axis=0, concat_axis=1, tiled=True)
    mixed = after + jnp.dot(
        returned.reshape(count, width), w_temporal_out, preferred_element_type=jnp.float32
    )
    return mixed.reshape(frames_here, rows, width).astype(jnp.bfloat16)


def solution(mesh):
    frame_n, row_n = mesh.devices.shape
    devices = mesh.devices.reshape(4, frame_n // 4, row_n // 4, 2, 2)
    fine = Mesh(devices, ("x", "zlo", "y", "zhi", "core"))
    grid_spec = P(("x", "zlo"), ("y", "zhi", "core"), None)
    in_specs = (grid_spec, P(), P(), P(), P(), P(), P())
    return jax.shard_map(layer, mesh=fine, in_specs=in_specs, out_specs=grid_spec, check_vma=False)
```

```python
import math

import jax
import jax.numpy as jnp
from jax import lax
from jax.experimental import pallas as pl
from jax.experimental.pallas import tpu as pltpu
from jax.sharding import Mesh

from jax.sharding import PartitionSpec as P

HEADS = 8


def layer_norm(rows, gain):
    mean = jnp.mean(rows, axis=-1, keepdims=True)
    centred = rows - mean
    spread = jnp.mean(centred * centred, axis=-1, keepdims=True)
    return centred * lax.rsqrt(spread + 1e-05) * gain


def _scores(q_ref, k_ref, cols, scale):
    return (
        lax.dot_general(
            q_ref[:, cols], k_ref[:, cols], (((1,), (1,)), ((), ())),
            preferred_element_type=jnp.float32,
        )
        * scale
    )


def partial_kernel(q_ref, k_ref, v_ref, o_ref, m_ref, l_ref, *, size, scale):
    for h in range(HEADS):
        cols = slice(h * size, (h + 1) * size)
        scores = _scores(q_ref, k_ref, cols, scale)
        peak = jnp.max(scores, axis=1, keepdims=True)
        weights = jnp.exp(scores - peak)
        l_ref[:, h : h + 1] = jnp.sum(weights, axis=1, keepdims=True)
        m_ref[:, h : h + 1] = peak
        o_ref[:, cols] = jnp.dot(
            weights.astype(jnp.bfloat16), v_ref[:, cols], preferred_element_type=jnp.float32
        )


def merge_kernel(q_ref, k_ref, v_ref, o1_ref, m1_ref, l1_ref, o_ref, m_ref, l_ref, *, size, scale):
    for h in range(HEADS):
        cols = slice(h * size, (h + 1) * size)
        scores = _scores(q_ref, k_ref, cols, scale)
        before = m1_ref[:, h : h + 1]
        peak = jnp.maximum(before, jnp.max(scores, axis=1, keepdims=True))
        weights = jnp.exp(scores - peak)
        fade = jnp.exp(before - peak)
        l_ref[:, h : h + 1] = l1_ref[:, h : h + 1] * fade + jnp.sum(weights, axis=1, keepdims=True)
        m_ref[:, h : h + 1] = peak
        o_ref[:, cols] = o1_ref[:, cols] * fade + jnp.dot(
            weights.astype(jnp.bfloat16), v_ref[:, cols], preferred_element_type=jnp.float32
        )


def _attention_call(kernel, query, keys, values, state):
    count, width = query.shape
    size = width // HEADS
    body = lambda *refs: kernel(*refs, size=size, scale=1.0 / math.sqrt(size))
    shapes = [
        jax.ShapeDtypeStruct((count, width), jnp.float32),
        jax.ShapeDtypeStruct((count, HEADS), jnp.float32),
        jax.ShapeDtypeStruct((count, HEADS), jnp.float32),
    ]
    return pl.pallas_call(
        body,
        out_shape=shapes,
        compiler_params=pltpu.CompilerParams(vmem_limit_bytes=48 * 1024 * 1024),
    )(query, keys, values, *state)


def spatial_partial(query, keys, values):
    return _attention_call(partial_kernel, query, keys, values, ())


def spatial_merge(query, keys, values, state):
    return _attention_call(merge_kernel, query, keys, values, state)


def spread_y(rows):
    ring = lax.axis_size("y")
    pieces = [rows]
    for shift in range(1, ring):
        pairs = [(i, (i + shift) % ring) for i in range(ring)]
        pieces.append(lax.ppermute(rows, "y", pairs))
    return jnp.concatenate(pieces, axis=0)


def attend_cells(block_qkv):
    frames, cells = (block_qkv.shape[0], block_qkv.shape[1])
    width = block_qkv.shape[2] // 3
    size = width // HEADS
    scale = 1.0 / math.sqrt(size)
    query = block_qkv[:, :, :width].reshape(frames, cells, HEADS, size)
    keys = block_qkv[:, :, width : 2 * width].reshape(frames, cells, HEADS, size)
    values = block_qkv[:, :, 2 * width :].reshape(frames, cells, HEADS, size)
    scores = jnp.einsum("fche,gche->chfg", query, keys, preferred_element_type=jnp.float32) * scale
    later = jnp.arange(frames)[:, None] >= jnp.arange(frames)[None, :]
    scores = jnp.where(later, scores, -1e30)
    peak = jnp.max(scores, axis=3, keepdims=True)
    weights = jnp.exp(scores - peak)
    total = jnp.sum(weights, axis=3)
    summed = jnp.einsum(
        "chfg,gche->fche", weights.astype(jnp.bfloat16), values, preferred_element_type=jnp.float32
    )
    context = summed / jnp.transpose(total, (2, 0, 1))[..., None]
    return context.reshape(frames, cells, width).astype(jnp.bfloat16)


def layer(
    tokens, norm_spatial, w_spatial, w_spatial_out, norm_temporal, w_temporal, w_temporal_out
):
    frames_here, rows, width = tokens.shape
    count = frames_here * rows
    resid = tokens.reshape(count, width).astype(jnp.float32)
    normed = layer_norm(resid, norm_spatial).astype(jnp.bfloat16)
    query = jnp.dot(normed, w_spatial[:, :width], preferred_element_type=jnp.float32).astype(
        jnp.bfloat16
    )
    partner = lax.ppermute(normed, "zhi", [(0, 1), (1, 0)])
    both = lax.all_gather(query, "core", axis=0, tiled=True)
    w_pairs = w_spatial[:, width:]
    near_rows = spread_y(normed)
    near = jnp.dot(near_rows, w_pairs, preferred_element_type=jnp.float32).astype(jnp.bfloat16)
    state = spatial_partial(both, near[:, :width], near[:, width:])
    far_rows = spread_y(partner)
    far = jnp.dot(far_rows, w_pairs, preferred_element_type=jnp.float32).astype(jnp.bfloat16)
    summed, peak, total = spatial_merge(both, far[:, :width], far[:, width:], state)
    mine = lax.axis_index("core")
    other = 1 - mine
    pick = lambda a, i: lax.dynamic_slice_in_dim(a, i * count, count, 0)
    packed = jnp.concatenate([pick(peak, other), pick(total, other)], axis=1)
    their_summed = lax.ppermute(pick(summed, other), "core", [(0, 1), (1, 0)])
    their_packed = lax.ppermute(packed, "core", [(0, 1), (1, 0)])
    own_peak, own_total, own_summed = pick(peak, mine), pick(total, mine), pick(summed, mine)
    their_peak, their_total = their_packed[:, :HEADS], their_packed[:, HEADS:]
    top = jnp.maximum(own_peak, their_peak)
    own_fade, their_fade = jnp.exp(own_peak - top), jnp.exp(their_peak - top)
    size = width // HEADS
    merged = (
        own_summed.reshape(count, HEADS, size) * own_fade[:, :, None]
        + their_summed.reshape(count, HEADS, size) * their_fade[:, :, None]
    )
    denominator = own_total * own_fade + their_total * their_fade
    context = (merged / denominator[:, :, None]).reshape(count, width).astype(jnp.bfloat16)
    after = resid + jnp.dot(context, w_spatial_out, preferred_element_type=jnp.float32)
    second = layer_norm(after, norm_temporal).astype(jnp.bfloat16)
    owners = lax.axis_size(("x", "zlo"))
    share = rows // owners
    second = second.reshape(frames_here, owners, share, width)
    gathered = lax.all_to_all(second, ("x", "zlo"), split_axis=1, concat_axis=0, tiled=True)
    frames_all = gathered.shape[0]
    qkv_t = jnp.dot(
        gathered.reshape(frames_all * share, width), w_temporal, preferred_element_type=jnp.float32
    ).astype(jnp.bfloat16)
    context_t = attend_cells(qkv_t.reshape(frames_all, share, 3 * width))
    context_t = context_t.reshape(frames_all, 1, share, width)
    returned = lax.all_to_all(context_t, ("x", "zlo"), split_axis=0, concat_axis=1, tiled=True)
    mixed = after + jnp.dot(
        returned.reshape(count, width), w_temporal_out, preferred_element_type=jnp.float32
    )
    return mixed.reshape(frames_here, rows, width).astype(jnp.bfloat16)


def solution(mesh):
    frame_n, row_n = mesh.devices.shape
    devices = mesh.devices.reshape(4, frame_n // 4, row_n // 4, 2, 2)
    fine = Mesh(devices, ("x", "zlo", "y", "zhi", "core"))
    grid_spec = P(("x", "zlo"), ("y", "zhi", "core"), None)
    in_specs = (grid_spec, P(), P(), P(), P(), P(), P())
    return jax.shard_map(layer, mesh=fine, in_specs=in_specs, out_specs=grid_spec, check_vma=False)
```

```python
import math

import jax
import jax.numpy as jnp
from jax import lax
from jax.experimental import pallas as pl
from jax.experimental.pallas import tpu as pltpu
from jax.sharding import Mesh

from jax.sharding import PartitionSpec as P

HEADS = 8


def layer_norm(rows, gain):
    mean = jnp.mean(rows, axis=-1, keepdims=True)
    centred = rows - mean
    spread = jnp.mean(centred * centred, axis=-1, keepdims=True)
    return centred * lax.rsqrt(spread + 1e-05) * gain


def _scores(q_ref, k_ref, cols, scale):
    del scale
    return lax.dot_general(
        q_ref[:, cols], k_ref[:, cols], (((1,), (1,)), ((), ())),
        preferred_element_type=jnp.float32,
    )


def partial_kernel(q_ref, k_ref, v_ref, o_ref, m_ref, l_ref, *, size, scale):
    for h in range(HEADS):
        cols = slice(h * size, (h + 1) * size)
        scores = _scores(q_ref, k_ref, cols, scale)
        peak = jnp.max(scores, axis=1, keepdims=True)
        weights = jnp.exp(scores - peak)
        l_ref[:, h : h + 1] = jnp.sum(weights, axis=1, keepdims=True)
        m_ref[:, h : h + 1] = peak
        o_ref[:, cols] = jnp.dot(
            weights.astype(jnp.bfloat16), v_ref[:, cols], preferred_element_type=jnp.float32
        )


def merge_kernel(q_ref, k_ref, v_ref, o1_ref, m1_ref, l1_ref, o_ref, m_ref, l_ref, *, size, scale):
    for h in range(HEADS):
        cols = slice(h * size, (h + 1) * size)
        scores = _scores(q_ref, k_ref, cols, scale)
        before = m1_ref[:, h : h + 1]
        peak = jnp.maximum(before, jnp.max(scores, axis=1, keepdims=True))
        weights = jnp.exp(scores - peak)
        fade = jnp.exp(before - peak)
        l_ref[:, h : h + 1] = l1_ref[:, h : h + 1] * fade + jnp.sum(weights, axis=1, keepdims=True)
        m_ref[:, h : h + 1] = peak
        o_ref[:, cols] = o1_ref[:, cols] * fade + jnp.dot(
            weights.astype(jnp.bfloat16), v_ref[:, cols], preferred_element_type=jnp.float32
        )


def _attention_call(kernel, query, keys, values, state):
    count, width = query.shape
    size = width // HEADS
    body = lambda *refs: kernel(*refs, size=size, scale=1.0 / math.sqrt(size))
    shapes = [
        jax.ShapeDtypeStruct((count, width), jnp.float32),
        jax.ShapeDtypeStruct((count, HEADS), jnp.float32),
        jax.ShapeDtypeStruct((count, HEADS), jnp.float32),
    ]
    return pl.pallas_call(
        body,
        out_shape=shapes,
        compiler_params=pltpu.CompilerParams(vmem_limit_bytes=48 * 1024 * 1024),
    )(query, keys, values, *state)


def combine_kernel(o1_ref, s1_ref, o2_ref, s2_ref, out_ref, *, size):
    for h in range(HEADS):
        cols = slice(h * size, (h + 1) * size)
        m1, l1 = s1_ref[:, h : h + 1], s1_ref[:, HEADS + h : HEADS + h + 1]
        m2, l2 = s2_ref[:, h : h + 1], s2_ref[:, HEADS + h : HEADS + h + 1]
        top = jnp.maximum(m1, m2)
        f1, f2 = jnp.exp(m1 - top), jnp.exp(m2 - top)
        summed = o1_ref[:, cols] * f1 + o2_ref[:, cols] * f2
        out_ref[:, cols] = (summed / (l1 * f1 + l2 * f2)).astype(out_ref.dtype)


def combine(own_summed, own_stats, their_summed, their_stats):
    count, width = own_summed.shape
    body = lambda *refs: combine_kernel(*refs, size=width // HEADS)
    return pl.pallas_call(body, out_shape=jax.ShapeDtypeStruct((count, width), jnp.bfloat16))(
        own_summed, own_stats, their_summed, their_stats
    )


def spatial_partial(query, keys, values):
    return _attention_call(partial_kernel, query, keys, values, ())


def spatial_merge(query, keys, values, state):
    return _attention_call(merge_kernel, query, keys, values, state)


def spread_y(rows):
    ring = lax.axis_size("y")
    pieces = [rows]
    for shift in range(1, ring):
        pairs = [(i, (i + shift) % ring) for i in range(ring)]
        pieces.append(lax.ppermute(rows, "y", pairs))
    return jnp.concatenate(pieces, axis=0)


def attend_cells(block_qkv):
    frames, cells = (block_qkv.shape[0], block_qkv.shape[1])
    width = block_qkv.shape[2] // 3
    size = width // HEADS
    scale = 1.0 / math.sqrt(size)
    query = block_qkv[:, :, :width].reshape(frames, cells, HEADS, size)
    keys = block_qkv[:, :, width : 2 * width].reshape(frames, cells, HEADS, size)
    values = block_qkv[:, :, 2 * width :].reshape(frames, cells, HEADS, size)
    del scale
    scores = jnp.einsum("fche,gche->chfg", query, keys, preferred_element_type=jnp.float32)
    later = jnp.arange(frames)[:, None] >= jnp.arange(frames)[None, :]
    scores = jnp.where(later, scores, -1e30)
    peak = jnp.max(scores, axis=3, keepdims=True)
    weights = jnp.exp(scores - peak)
    total = jnp.sum(weights, axis=3)
    summed = jnp.einsum(
        "chfg,gche->fche", weights.astype(jnp.bfloat16), values, preferred_element_type=jnp.float32
    )
    context = summed / jnp.transpose(total, (2, 0, 1))[..., None]
    return context.reshape(frames, cells, width).astype(jnp.bfloat16)


def layer(
    tokens, norm_spatial, w_spatial, w_spatial_out, norm_temporal, w_temporal, w_temporal_out
):
    frames_here, rows, width = tokens.shape
    count = frames_here * rows
    resid = tokens.reshape(count, width).astype(jnp.float32)
    normed = layer_norm(resid, norm_spatial).astype(jnp.bfloat16)
    w_query = w_spatial[:, :width] * jnp.asarray(1.0 / math.sqrt(width // HEADS), w_spatial.dtype)
    query = jnp.dot(normed, w_query, preferred_element_type=jnp.float32).astype(jnp.bfloat16)
    partner = lax.ppermute(normed, "zhi", [(0, 1), (1, 0)])
    both = lax.all_gather(query, "core", axis=0, tiled=True)
    w_pairs = w_spatial[:, width:]
    near_rows = spread_y(normed)
    near = jnp.dot(near_rows, w_pairs, preferred_element_type=jnp.float32).astype(jnp.bfloat16)
    state = spatial_partial(both, near[:, :width], near[:, width:])
    far_rows = spread_y(partner)
    far = jnp.dot(far_rows, w_pairs, preferred_element_type=jnp.float32).astype(jnp.bfloat16)
    summed, peak, total = spatial_merge(both, far[:, :width], far[:, width:], state)
    mine = lax.axis_index("core")
    other = 1 - mine
    pick = lambda a, i: lax.dynamic_slice_in_dim(a, i * count, count, 0)
    stats = jnp.concatenate([peak, total], axis=1)
    their_summed = lax.ppermute(pick(summed, other), "core", [(0, 1), (1, 0)])
    their_stats = lax.ppermute(pick(stats, other), "core", [(0, 1), (1, 0)])
    context = combine(pick(summed, mine), pick(stats, mine), their_summed, their_stats)
    after = resid + jnp.dot(context, w_spatial_out, preferred_element_type=jnp.float32)
    second = layer_norm(after, norm_temporal).astype(jnp.bfloat16)
    owners = lax.axis_size(("x", "zlo"))
    share = rows // owners
    second = second.reshape(frames_here, owners, share, width)
    gathered = lax.all_to_all(second, ("x", "zlo"), split_axis=1, concat_axis=0, tiled=True)
    frames_all = gathered.shape[0]
    w_temporal = w_temporal.at[:, :width].multiply(
        jnp.asarray(1.0 / math.sqrt(width // HEADS), w_temporal.dtype)
    )
    qkv_t = jnp.dot(
        gathered.reshape(frames_all * share, width), w_temporal, preferred_element_type=jnp.float32
    ).astype(jnp.bfloat16)
    context_t = attend_cells(qkv_t.reshape(frames_all, share, 3 * width))
    context_t = context_t.reshape(frames_all, 1, share, width)
    returned = lax.all_to_all(context_t, ("x", "zlo"), split_axis=0, concat_axis=1, tiled=True)
    mixed = after + jnp.dot(
        returned.reshape(count, width), w_temporal_out, preferred_element_type=jnp.float32
    )
    return mixed.reshape(frames_here, rows, width).astype(jnp.bfloat16)


def solution(mesh):
    frame_n, row_n = mesh.devices.shape
    devices = mesh.devices.reshape(4, frame_n // 4, row_n // 4, 2, 2)
    fine = Mesh(devices, ("x", "zlo", "y", "zhi", "core"))
    grid_spec = P(("x", "zlo"), ("y", "zhi", "core"), None)
    in_specs = (grid_spec, P(), P(), P(), P(), P(), P())
    return jax.shard_map(layer, mesh=fine, in_specs=in_specs, out_specs=grid_spec, check_vma=False)
```

```python
import math

import jax
import jax.numpy as jnp
from jax import lax
from jax.experimental import pallas as pl
from jax.experimental.pallas import tpu as pltpu
from jax.sharding import Mesh

from jax.sharding import PartitionSpec as P

HEADS = 8


def layer_norm(rows, gain):
    mean = jnp.mean(rows, axis=-1, keepdims=True)
    centred = rows - mean
    spread = jnp.mean(centred * centred, axis=-1, keepdims=True)
    return centred * lax.rsqrt(spread + 1e-05) * gain


def _scores(q_ref, k_ref, cols, scale):
    del scale
    return lax.dot_general(
        q_ref[:, cols], k_ref[:, cols], (((1,), (1,)), ((), ())),
        preferred_element_type=jnp.float32,
    )


def partial_kernel(q_ref, k_ref, v_ref, o_ref, m_ref, l_ref, *, size, scale):
    for h in range(HEADS):
        cols = slice(h * size, (h + 1) * size)
        scores = _scores(q_ref, k_ref, cols, scale)
        peak = jnp.max(scores, axis=1, keepdims=True)
        weights = jnp.exp(scores - peak)
        l_ref[:, h : h + 1] = jnp.sum(weights, axis=1, keepdims=True)
        m_ref[:, h : h + 1] = peak
        o_ref[:, cols] = jnp.dot(
            weights.astype(jnp.bfloat16), v_ref[:, cols], preferred_element_type=jnp.float32
        )


def merge_kernel(q_ref, k_ref, v_ref, o1_ref, m1_ref, l1_ref, out_ref, *, size, rows):
    width = HEADS * size
    for h in range(HEADS):
        cols = slice(h * size, (h + 1) * size)
        scores = lax.dot_general(
            q_ref[rows, cols], k_ref[:, cols], (((1,), (1,)), ((), ())),
            preferred_element_type=jnp.float32,
        )
        before = m1_ref[rows, h : h + 1]
        peak = jnp.maximum(before, jnp.max(scores, axis=1, keepdims=True))
        weights = jnp.exp(scores - peak)
        fade = jnp.exp(before - peak)
        total = l1_ref[rows, h : h + 1] * fade + jnp.sum(weights, axis=1, keepdims=True)
        out_ref[:, cols] = o1_ref[rows, cols] * fade + jnp.dot(
            weights.astype(jnp.bfloat16), v_ref[:, cols], preferred_element_type=jnp.float32
        )
        out_ref[:, width + h : width + h + 1] = peak
        out_ref[:, width + HEADS + h : width + HEADS + h + 1] = total


def _attention_call(kernel, query, keys, values, state):
    count, width = query.shape
    size = width // HEADS
    body = lambda *refs: kernel(*refs, size=size, scale=1.0 / math.sqrt(size))
    shapes = [
        jax.ShapeDtypeStruct((count, width), jnp.float32),
        jax.ShapeDtypeStruct((count, HEADS), jnp.float32),
        jax.ShapeDtypeStruct((count, HEADS), jnp.float32),
    ]
    return pl.pallas_call(
        body,
        out_shape=shapes,
        compiler_params=pltpu.CompilerParams(vmem_limit_bytes=48 * 1024 * 1024),
    )(query, keys, values, *state)


def combine_kernel(a_ref, b_ref, out_ref, *, size):
    width = HEADS * size
    for h in range(HEADS):
        cols = slice(h * size, (h + 1) * size)
        m1, m2 = a_ref[:, width + h : width + h + 1], b_ref[:, width + h : width + h + 1]
        l1 = a_ref[:, width + HEADS + h : width + HEADS + h + 1]
        l2 = b_ref[:, width + HEADS + h : width + HEADS + h + 1]
        top = jnp.maximum(m1, m2)
        f1, f2 = jnp.exp(m1 - top), jnp.exp(m2 - top)
        summed = a_ref[:, cols] * f1 + b_ref[:, cols] * f2
        out_ref[:, cols] = (summed / (l1 * f1 + l2 * f2)).astype(out_ref.dtype)


def combine(own, theirs):
    count, packed = own.shape
    width = packed - 2 * HEADS
    body = lambda *refs: combine_kernel(*refs, size=width // HEADS)
    return pl.pallas_call(body, out_shape=jax.ShapeDtypeStruct((count, width), jnp.bfloat16))(
        own, theirs
    )


def spatial_partial(query, keys, values):
    return _attention_call(partial_kernel, query, keys, values, ())


def spatial_merge(query, keys, values, state, start, count):
    width = query.shape[1]
    size = width // HEADS
    body = lambda *refs: merge_kernel(*refs, size=size, rows=slice(start, start + count))
    return pl.pallas_call(
        body,
        out_shape=jax.ShapeDtypeStruct((count, width + 2 * HEADS), jnp.float32),
        compiler_params=pltpu.CompilerParams(vmem_limit_bytes=48 * 1024 * 1024),
    )(query, keys, values, *state)


def spread_y(rows):
    ring = lax.axis_size("y")
    pieces = [rows]
    for shift in range(1, ring):
        pairs = [(i, (i + shift) % ring) for i in range(ring)]
        pieces.append(lax.ppermute(rows, "y", pairs))
    return jnp.concatenate(pieces, axis=0)


def attend_cells(block_qkv):
    frames, cells = (block_qkv.shape[0], block_qkv.shape[1])
    width = block_qkv.shape[2] // 3
    size = width // HEADS
    scale = 1.0 / math.sqrt(size)
    query = block_qkv[:, :, :width].reshape(frames, cells, HEADS, size)
    keys = block_qkv[:, :, width : 2 * width].reshape(frames, cells, HEADS, size)
    values = block_qkv[:, :, 2 * width :].reshape(frames, cells, HEADS, size)
    del scale
    scores = jnp.einsum("fche,gche->chfg", query, keys, preferred_element_type=jnp.float32)
    later = jnp.arange(frames)[:, None] >= jnp.arange(frames)[None, :]
    scores = jnp.where(later, scores, -1e30)
    peak = jnp.max(scores, axis=3, keepdims=True)
    weights = jnp.exp(scores - peak)
    total = jnp.sum(weights, axis=3)
    summed = jnp.einsum(
        "chfg,gche->fche", weights.astype(jnp.bfloat16), values, preferred_element_type=jnp.float32
    )
    context = summed / jnp.transpose(total, (2, 0, 1))[..., None]
    return context.reshape(frames, cells, width).astype(jnp.bfloat16)


def layer(
    tokens, norm_spatial, w_spatial, w_spatial_out, norm_temporal, w_temporal, w_temporal_out
):
    frames_here, rows, width = tokens.shape
    count = frames_here * rows
    resid = tokens.reshape(count, width).astype(jnp.float32)
    normed = layer_norm(resid, norm_spatial).astype(jnp.bfloat16)
    w_query = w_spatial[:, :width] * jnp.asarray(1.0 / math.sqrt(width // HEADS), w_spatial.dtype)
    query = jnp.dot(normed, w_query, preferred_element_type=jnp.float32).astype(jnp.bfloat16)
    partner = lax.ppermute(normed, "zhi", [(0, 1), (1, 0)])
    swap = [(0, 1), (1, 0)]
    both = jnp.concatenate([lax.ppermute(query, "core", swap), query], axis=0)
    w_pairs = w_spatial[:, width:]
    near_rows = spread_y(normed)
    near = jnp.dot(near_rows, w_pairs, preferred_element_type=jnp.float32).astype(jnp.bfloat16)
    state = spatial_partial(both, near[:, :width], near[:, width:])
    far_rows = spread_y(partner)
    far = jnp.dot(far_rows, w_pairs, preferred_element_type=jnp.float32).astype(jnp.bfloat16)
    theirs = spatial_merge(both, far[:, :width], far[:, width:], state, 0, count)
    theirs = lax.ppermute(theirs, "core", swap)
    own = spatial_merge(both, far[:, :width], far[:, width:], state, count, count)
    context = combine(own, theirs)
    after = resid + jnp.dot(context, w_spatial_out, preferred_element_type=jnp.float32)
    second = layer_norm(after, norm_temporal).astype(jnp.bfloat16)
    owners = lax.axis_size(("x", "zlo"))
    share = rows // owners
    second = second.reshape(frames_here, owners, share, width)
    gathered = lax.all_to_all(second, ("x", "zlo"), split_axis=1, concat_axis=0, tiled=True)
    frames_all = gathered.shape[0]
    w_temporal = w_temporal.at[:, :width].multiply(
        jnp.asarray(1.0 / math.sqrt(width // HEADS), w_temporal.dtype)
    )
    qkv_t = jnp.dot(
        gathered.reshape(frames_all * share, width), w_temporal, preferred_element_type=jnp.float32
    ).astype(jnp.bfloat16)
    context_t = attend_cells(qkv_t.reshape(frames_all, share, 3 * width))
    context_t = context_t.reshape(frames_all, 1, share, width)
    returned = lax.all_to_all(context_t, ("x", "zlo"), split_axis=0, concat_axis=1, tiled=True)
    mixed = after + jnp.dot(
        returned.reshape(count, width), w_temporal_out, preferred_element_type=jnp.float32
    )
    return mixed.reshape(frames_here, rows, width).astype(jnp.bfloat16)


def solution(mesh):
    frame_n, row_n = mesh.devices.shape
    devices = mesh.devices.reshape(4, frame_n // 4, row_n // 4, 2, 2)
    fine = Mesh(devices, ("x", "zlo", "y", "zhi", "core"))
    grid_spec = P(("x", "zlo"), ("y", "zhi", "core"), None)
    in_specs = (grid_spec, P(), P(), P(), P(), P(), P())
    return jax.shard_map(layer, mesh=fine, in_specs=in_specs, out_specs=grid_spec, check_vma=False)
```

```python
import math

import jax
import jax.numpy as jnp
from jax import lax
from jax.experimental import pallas as pl
from jax.experimental.pallas import tpu as pltpu
from jax.sharding import Mesh

from jax.sharding import PartitionSpec as P

HEADS = 8
STATS = 64


def layer_norm(rows, gain):
    mean = jnp.mean(rows, axis=-1, keepdims=True)
    centred = rows - mean
    spread = jnp.mean(centred * centred, axis=-1, keepdims=True)
    return centred * lax.rsqrt(spread + 1e-05) * gain


def _scores(q_ref, k_ref, cols, scale):
    del scale
    return lax.dot_general(
        q_ref[:, cols], k_ref[:, cols], (((1,), (1,)), ((), ())),
        preferred_element_type=jnp.float32,
    )


def partial_kernel(q_ref, k_ref, v_ref, o_ref, m_ref, l_ref, *, size, scale):
    for h in range(HEADS):
        cols = slice(h * size, (h + 1) * size)
        scores = _scores(q_ref, k_ref, cols, scale)
        peak = jnp.max(scores, axis=1, keepdims=True)
        weights = jnp.exp(scores - peak)
        l_ref[:, h : h + 1] = jnp.sum(weights, axis=1, keepdims=True)
        m_ref[:, h : h + 1] = peak
        o_ref[:, cols] = jnp.dot(
            weights.astype(jnp.bfloat16), v_ref[:, cols], preferred_element_type=jnp.float32
        )


def merge_kernel(q_ref, k_ref, v_ref, o1_ref, m1_ref, l1_ref, out_ref, *, size, rows):
    width = HEADS * size
    for h in range(HEADS):
        cols = slice(h * size, (h + 1) * size)
        scores = lax.dot_general(
            q_ref[rows, cols], k_ref[:, cols], (((1,), (1,)), ((), ())),
            preferred_element_type=jnp.float32,
        )
        before = m1_ref[rows, h : h + 1]
        peak = jnp.maximum(before, jnp.max(scores, axis=1, keepdims=True))
        weights = jnp.exp(scores - peak)
        fade = jnp.exp(before - peak)
        total = l1_ref[rows, h : h + 1] * fade + jnp.sum(weights, axis=1, keepdims=True)
        out_ref[:, cols] = o1_ref[rows, cols] * fade + jnp.dot(
            weights.astype(jnp.bfloat16), v_ref[:, cols], preferred_element_type=jnp.float32
        )
        out_ref[:, width + h : width + h + 1] = peak
        out_ref[:, width + STATS + h : width + STATS + h + 1] = total


def _attention_call(kernel, query, keys, values, state):
    count, width = query.shape
    size = width // HEADS
    body = lambda *refs: kernel(*refs, size=size, scale=1.0 / math.sqrt(size))
    shapes = [
        jax.ShapeDtypeStruct((count, width), jnp.float32),
        jax.ShapeDtypeStruct((count, HEADS), jnp.float32),
        jax.ShapeDtypeStruct((count, HEADS), jnp.float32),
    ]
    return pl.pallas_call(
        body,
        out_shape=shapes,
        compiler_params=pltpu.CompilerParams(vmem_limit_bytes=48 * 1024 * 1024),
    )(query, keys, values, *state)


def combine_kernel(a_ref, b_ref, out_ref, *, size):
    width = HEADS * size
    for h in range(HEADS):
        cols = slice(h * size, (h + 1) * size)
        m1, m2 = a_ref[:, width + h : width + h + 1], b_ref[:, width + h : width + h + 1]
        l1 = a_ref[:, width + STATS + h : width + STATS + h + 1]
        l2 = b_ref[:, width + STATS + h : width + STATS + h + 1]
        top = jnp.maximum(m1, m2)
        f1, f2 = jnp.exp(m1 - top), jnp.exp(m2 - top)
        summed = a_ref[:, cols] * f1 + b_ref[:, cols] * f2
        out_ref[:, cols] = (summed / (l1 * f1 + l2 * f2)).astype(out_ref.dtype)


def combine(own, theirs):
    count, packed = own.shape
    width = packed - 2 * STATS
    body = lambda *refs: combine_kernel(*refs, size=width // HEADS)
    return pl.pallas_call(body, out_shape=jax.ShapeDtypeStruct((count, width), jnp.bfloat16))(
        own, theirs
    )


def spatial_partial(query, keys, values):
    return _attention_call(partial_kernel, query, keys, values, ())


def spatial_merge(query, keys, values, state, start, count):
    width = query.shape[1]
    size = width // HEADS
    body = lambda *refs: merge_kernel(*refs, size=size, rows=slice(start, start + count))
    return pl.pallas_call(
        body,
        out_shape=jax.ShapeDtypeStruct((count, width + 2 * STATS), jnp.float32),
        compiler_params=pltpu.CompilerParams(vmem_limit_bytes=48 * 1024 * 1024),
    )(query, keys, values, *state)


def spread_y(rows):
    ring = lax.axis_size("y")
    pieces = [rows]
    for shift in range(1, ring):
        pairs = [(i, (i + shift) % ring) for i in range(ring)]
        pieces.append(lax.ppermute(rows, "y", pairs))
    return jnp.concatenate(pieces, axis=0)


def attend_cells(block_qkv):
    frames, cells = (block_qkv.shape[0], block_qkv.shape[1])
    width = block_qkv.shape[2] // 3
    size = width // HEADS
    scale = 1.0 / math.sqrt(size)
    query = block_qkv[:, :, :width].reshape(frames, cells, HEADS, size)
    keys = block_qkv[:, :, width : 2 * width].reshape(frames, cells, HEADS, size)
    values = block_qkv[:, :, 2 * width :].reshape(frames, cells, HEADS, size)
    del scale
    scores = jnp.einsum("fche,gche->chfg", query, keys, preferred_element_type=jnp.float32)
    later = jnp.arange(frames)[:, None] >= jnp.arange(frames)[None, :]
    scores = jnp.where(later, scores, -1e30)
    peak = jnp.max(scores, axis=3, keepdims=True)
    weights = jnp.exp(scores - peak)
    total = jnp.sum(weights, axis=3)
    summed = jnp.einsum(
        "chfg,gche->fche", weights.astype(jnp.bfloat16), values, preferred_element_type=jnp.float32
    )
    context = summed / jnp.transpose(total, (2, 0, 1))[..., None]
    return context.reshape(frames, cells, width).astype(jnp.bfloat16)


def layer(
    tokens, norm_spatial, w_spatial, w_spatial_out, norm_temporal, w_temporal, w_temporal_out
):
    frames_here, rows, width = tokens.shape
    count = frames_here * rows
    resid = tokens.reshape(count, width).astype(jnp.float32)
    normed = layer_norm(resid, norm_spatial).astype(jnp.bfloat16)
    w_query = w_spatial[:, :width] * jnp.asarray(1.0 / math.sqrt(width // HEADS), w_spatial.dtype)
    query = jnp.dot(normed, w_query, preferred_element_type=jnp.float32).astype(jnp.bfloat16)
    partner = lax.ppermute(normed, "zhi", [(0, 1), (1, 0)])
    swap = [(0, 1), (1, 0)]
    both = jnp.concatenate([lax.ppermute(query, "core", swap), query], axis=0)
    w_pairs = w_spatial[:, width:]
    near_rows = spread_y(normed)
    near = jnp.dot(near_rows, w_pairs, preferred_element_type=jnp.float32).astype(jnp.bfloat16)
    state = spatial_partial(both, near[:, :width], near[:, width:])
    far_rows = spread_y(partner)
    far = jnp.dot(far_rows, w_pairs, preferred_element_type=jnp.float32).astype(jnp.bfloat16)
    theirs = spatial_merge(both, far[:, :width], far[:, width:], state, 0, count)
    theirs = lax.ppermute(theirs, "core", swap)
    own = spatial_merge(both, far[:, :width], far[:, width:], state, count, count)
    context = combine(own, theirs)
    after = resid + jnp.dot(context, w_spatial_out, preferred_element_type=jnp.float32)
    second = layer_norm(after, norm_temporal).astype(jnp.bfloat16)
    owners = lax.axis_size(("x", "zlo"))
    share = rows // owners
    second = second.reshape(frames_here, owners, share, width)
    gathered = lax.all_to_all(second, ("x", "zlo"), split_axis=1, concat_axis=0, tiled=True)
    frames_all = gathered.shape[0]
    w_temporal = w_temporal.at[:, :width].multiply(
        jnp.asarray(1.0 / math.sqrt(width // HEADS), w_temporal.dtype)
    )
    qkv_t = jnp.dot(
        gathered.reshape(frames_all * share, width), w_temporal, preferred_element_type=jnp.float32
    ).astype(jnp.bfloat16)
    context_t = attend_cells(qkv_t.reshape(frames_all, share, 3 * width))
    context_t = context_t.reshape(frames_all, 1, share, width)
    returned = lax.all_to_all(context_t, ("x", "zlo"), split_axis=0, concat_axis=1, tiled=True)
    mixed = after + jnp.dot(
        returned.reshape(count, width), w_temporal_out, preferred_element_type=jnp.float32
    )
    return mixed.reshape(frames_here, rows, width).astype(jnp.bfloat16)


def solution(mesh):
    frame_n, row_n = mesh.devices.shape
    devices = mesh.devices.reshape(4, frame_n // 4, row_n // 4, 2, 2)
    fine = Mesh(devices, ("x", "zlo", "y", "zhi", "core"))
    grid_spec = P(("x", "zlo"), ("y", "zhi", "core"), None)
    in_specs = (grid_spec, P(), P(), P(), P(), P(), P())
    return jax.shard_map(layer, mesh=fine, in_specs=in_specs, out_specs=grid_spec, check_vma=False)
```

```python
import math

import jax
import jax.numpy as jnp
from jax import lax
from jax.experimental import pallas as pl
from jax.experimental.pallas import tpu as pltpu
from jax.sharding import Mesh

from jax.sharding import PartitionSpec as P

HEADS = 8
STATS = 64


def layer_norm(rows, gain):
    mean = jnp.mean(rows, axis=-1, keepdims=True)
    centred = rows - mean
    spread = jnp.mean(centred * centred, axis=-1, keepdims=True)
    return centred * lax.rsqrt(spread + 1e-05) * gain


def _scores(q_ref, k_ref, cols, scale):
    del scale
    return lax.dot_general(
        q_ref[:, cols], k_ref[:, cols], (((1,), (1,)), ((), ())),
        preferred_element_type=jnp.float32,
    )


def partial_kernel(q_ref, k_ref, v_ref, o_ref, m_ref, l_ref, *, size, scale):
    for h in range(HEADS):
        cols = slice(h * size, (h + 1) * size)
        scores = _scores(q_ref, k_ref, cols, scale)
        peak = jnp.max(scores, axis=1, keepdims=True)
        weights = jnp.exp(scores - peak)
        l_ref[:, h : h + 1] = jnp.sum(weights, axis=1, keepdims=True)
        m_ref[:, h : h + 1] = peak
        o_ref[:, cols] = jnp.dot(
            weights.astype(jnp.bfloat16), v_ref[:, cols], preferred_element_type=jnp.float32
        )


def merge_kernel(q_ref, k_ref, v_ref, o1_ref, m1_ref, l1_ref, out_ref, *, size, rows):
    width = HEADS * size
    for h in range(HEADS):
        cols = slice(h * size, (h + 1) * size)
        scores = lax.dot_general(
            q_ref[rows, cols], k_ref[:, cols], (((1,), (1,)), ((), ())),
            preferred_element_type=jnp.float32,
        )
        before = m1_ref[rows, h : h + 1]
        peak = jnp.maximum(before, jnp.max(scores, axis=1, keepdims=True))
        weights = jnp.exp(scores - peak)
        fade = jnp.exp(before - peak)
        total = l1_ref[rows, h : h + 1] * fade + jnp.sum(weights, axis=1, keepdims=True)
        out_ref[:, cols] = o1_ref[rows, cols] * fade + jnp.dot(
            weights.astype(jnp.bfloat16), v_ref[:, cols], preferred_element_type=jnp.float32
        )
        out_ref[:, width + h : width + h + 1] = peak
        out_ref[:, width + STATS + h : width + STATS + h + 1] = total


def _attention_call(kernel, query, keys, values, state):
    count, width = query.shape
    size = width // HEADS
    body = lambda *refs: kernel(*refs, size=size, scale=1.0 / math.sqrt(size))
    shapes = [
        jax.ShapeDtypeStruct((count, width), jnp.float32),
        jax.ShapeDtypeStruct((count, HEADS), jnp.float32),
        jax.ShapeDtypeStruct((count, HEADS), jnp.float32),
    ]
    return pl.pallas_call(
        body,
        out_shape=shapes,
        compiler_params=pltpu.CompilerParams(vmem_limit_bytes=48 * 1024 * 1024),
    )(query, keys, values, *state)


def final_kernel(q_ref, k_ref, v_ref, o1_ref, m1_ref, l1_ref, t_ref, out_ref, *, size, rows):
    width = HEADS * size
    for h in range(HEADS):
        cols = slice(h * size, (h + 1) * size)
        scores = lax.dot_general(
            q_ref[rows, cols], k_ref[:, cols], (((1,), (1,)), ((), ())),
            preferred_element_type=jnp.float32,
        )
        before = m1_ref[rows, h : h + 1]
        theirs = t_ref[:, width + h : width + h + 1]
        top = jnp.maximum(jnp.maximum(before, theirs), jnp.max(scores, axis=1, keepdims=True))
        weights = jnp.exp(scores - top)
        fade, their_fade = jnp.exp(before - top), jnp.exp(theirs - top)
        total = (
            l1_ref[rows, h : h + 1] * fade
            + t_ref[:, width + STATS + h : width + STATS + h + 1] * their_fade
            + jnp.sum(weights, axis=1, keepdims=True)
        )
        summed = (
            o1_ref[rows, cols] * fade
            + t_ref[:, cols] * their_fade
            + jnp.dot(weights.astype(jnp.bfloat16), v_ref[:, cols], preferred_element_type=jnp.float32)
        )
        out_ref[:, cols] = (summed / total).astype(out_ref.dtype)


def spatial_final(query, keys, values, state, theirs, start, count):
    width = query.shape[1]
    body = lambda *refs: final_kernel(
        *refs, size=width // HEADS, rows=slice(start, start + count)
    )
    return pl.pallas_call(
        body,
        out_shape=jax.ShapeDtypeStruct((count, width), jnp.bfloat16),
        compiler_params=pltpu.CompilerParams(vmem_limit_bytes=48 * 1024 * 1024),
    )(query, keys, values, *state, theirs)


def spatial_partial(query, keys, values):
    return _attention_call(partial_kernel, query, keys, values, ())


def spatial_merge(query, keys, values, state, start, count):
    width = query.shape[1]
    size = width // HEADS
    body = lambda *refs: merge_kernel(*refs, size=size, rows=slice(start, start + count))
    return pl.pallas_call(
        body,
        out_shape=jax.ShapeDtypeStruct((count, width + 2 * STATS), jnp.float32),
        compiler_params=pltpu.CompilerParams(vmem_limit_bytes=48 * 1024 * 1024),
    )(query, keys, values, *state)


def spread_y(rows):
    ring = lax.axis_size("y")
    pieces = [rows]
    for shift in range(1, ring):
        pairs = [(i, (i + shift) % ring) for i in range(ring)]
        pieces.append(lax.ppermute(rows, "y", pairs))
    return jnp.concatenate(pieces, axis=0)


def attend_cells(block_qkv):
    frames, cells = (block_qkv.shape[0], block_qkv.shape[1])
    width = block_qkv.shape[2] // 3
    size = width // HEADS
    scale = 1.0 / math.sqrt(size)
    query = block_qkv[:, :, :width].reshape(frames, cells, HEADS, size)
    keys = block_qkv[:, :, width : 2 * width].reshape(frames, cells, HEADS, size)
    values = block_qkv[:, :, 2 * width :].reshape(frames, cells, HEADS, size)
    del scale
    scores = jnp.einsum("fche,gche->chfg", query, keys, preferred_element_type=jnp.float32)
    later = jnp.arange(frames)[:, None] >= jnp.arange(frames)[None, :]
    scores = jnp.where(later, scores, -1e30)
    peak = jnp.max(scores, axis=3, keepdims=True)
    weights = jnp.exp(scores - peak)
    total = jnp.sum(weights, axis=3)
    summed = jnp.einsum(
        "chfg,gche->fche", weights.astype(jnp.bfloat16), values, preferred_element_type=jnp.float32
    )
    context = summed / jnp.transpose(total, (2, 0, 1))[..., None]
    return context.reshape(frames, cells, width).astype(jnp.bfloat16)


def layer(
    tokens, norm_spatial, w_spatial, w_spatial_out, norm_temporal, w_temporal, w_temporal_out
):
    frames_here, rows, width = tokens.shape
    count = frames_here * rows
    resid = tokens.reshape(count, width).astype(jnp.float32)
    normed = layer_norm(resid, norm_spatial).astype(jnp.bfloat16)
    w_query = w_spatial[:, :width] * jnp.asarray(1.0 / math.sqrt(width // HEADS), w_spatial.dtype)
    query = jnp.dot(normed, w_query, preferred_element_type=jnp.float32).astype(jnp.bfloat16)
    partner = lax.ppermute(normed, "zhi", [(0, 1), (1, 0)])
    swap = [(0, 1), (1, 0)]
    both = jnp.concatenate([lax.ppermute(query, "core", swap), query], axis=0)
    w_pairs = w_spatial[:, width:]
    near_rows = spread_y(normed)
    near = jnp.dot(near_rows, w_pairs, preferred_element_type=jnp.float32).astype(jnp.bfloat16)
    state = spatial_partial(both, near[:, :width], near[:, width:])
    far_rows = spread_y(partner)
    far = jnp.dot(far_rows, w_pairs, preferred_element_type=jnp.float32).astype(jnp.bfloat16)
    theirs = spatial_merge(both, far[:, :width], far[:, width:], state, 0, count)
    theirs = lax.ppermute(theirs, "core", swap)
    context = spatial_final(both, far[:, :width], far[:, width:], state, theirs, count, count)
    after = resid + jnp.dot(context, w_spatial_out, preferred_element_type=jnp.float32)
    second = layer_norm(after, norm_temporal).astype(jnp.bfloat16)
    owners = lax.axis_size(("x", "zlo"))
    share = rows // owners
    second = second.reshape(frames_here, owners, share, width)
    gathered = lax.all_to_all(second, ("x", "zlo"), split_axis=1, concat_axis=0, tiled=True)
    frames_all = gathered.shape[0]
    w_temporal = w_temporal.at[:, :width].multiply(
        jnp.asarray(1.0 / math.sqrt(width // HEADS), w_temporal.dtype)
    )
    qkv_t = jnp.dot(
        gathered.reshape(frames_all * share, width), w_temporal, preferred_element_type=jnp.float32
    ).astype(jnp.bfloat16)
    context_t = attend_cells(qkv_t.reshape(frames_all, share, 3 * width))
    context_t = context_t.reshape(frames_all, 1, share, width)
    returned = lax.all_to_all(context_t, ("x", "zlo"), split_axis=0, concat_axis=1, tiled=True)
    mixed = after + jnp.dot(
        returned.reshape(count, width), w_temporal_out, preferred_element_type=jnp.float32
    )
    return mixed.reshape(frames_here, rows, width).astype(jnp.bfloat16)


def solution(mesh):
    frame_n, row_n = mesh.devices.shape
    devices = mesh.devices.reshape(4, frame_n // 4, row_n // 4, 2, 2)
    fine = Mesh(devices, ("x", "zlo", "y", "zhi", "core"))
    grid_spec = P(("x", "zlo"), ("y", "zhi", "core"), None)
    in_specs = (grid_spec, P(), P(), P(), P(), P(), P())
    return jax.shard_map(layer, mesh=fine, in_specs=in_specs, out_specs=grid_spec, check_vma=False)
```

```python
import math

import jax
import jax.numpy as jnp
from jax import lax
from jax.experimental import pallas as pl
from jax.experimental.pallas import tpu as pltpu
from jax.sharding import Mesh

from jax.sharding import PartitionSpec as P

HEADS = 8
STATS = 64


def layer_norm(rows, gain):
    mean = jnp.mean(rows, axis=-1, keepdims=True)
    centred = rows - mean
    spread = jnp.mean(centred * centred, axis=-1, keepdims=True)
    return centred * lax.rsqrt(spread + 1e-05) * gain


def _scores(q_ref, k_ref, cols, scale):
    del scale
    return lax.dot_general(
        q_ref[:, cols], k_ref[:, cols], (((1,), (1,)), ((), ())),
        preferred_element_type=jnp.float32,
    )


def partial_kernel(q_ref, k_ref, v_ref, o_ref, m_ref, l_ref, *, size, scale):
    for h in range(HEADS):
        cols = slice(h * size, (h + 1) * size)
        scores = _scores(q_ref, k_ref, cols, scale)
        peak = jnp.max(scores, axis=1, keepdims=True)
        weights = jnp.exp(scores - peak)
        l_ref[:, h : h + 1] = jnp.sum(weights, axis=1, keepdims=True)
        m_ref[:, h : h + 1] = peak
        o_ref[:, cols] = jnp.dot(
            weights.astype(jnp.bfloat16), v_ref[:, cols], preferred_element_type=jnp.float32
        )


def merge_kernel(q_ref, k_ref, v_ref, o1_ref, m1_ref, l1_ref, out_ref, *, size, rows):
    width = HEADS * size
    for h in range(HEADS):
        cols = slice(h * size, (h + 1) * size)
        scores = lax.dot_general(
            q_ref[rows, cols], k_ref[:, cols], (((1,), (1,)), ((), ())),
            preferred_element_type=jnp.float32,
        )
        before = m1_ref[rows, h : h + 1]
        peak = jnp.maximum(before, jnp.max(scores, axis=1, keepdims=True))
        weights = jnp.exp(scores - peak)
        fade = jnp.exp(before - peak)
        total = l1_ref[rows, h : h + 1] * fade + jnp.sum(weights, axis=1, keepdims=True)
        out_ref[:, cols] = o1_ref[rows, cols] * fade + jnp.dot(
            weights.astype(jnp.bfloat16), v_ref[:, cols], preferred_element_type=jnp.float32
        )
        out_ref[:, width + h : width + h + 1] = peak
        out_ref[:, width + STATS + h : width + STATS + h + 1] = total


def _attention_call(kernel, query, keys, values, state):
    count, width = query.shape
    size = width // HEADS
    body = lambda *refs: kernel(*refs, size=size, scale=1.0 / math.sqrt(size))
    shapes = [
        jax.ShapeDtypeStruct((count, width), jnp.float32),
        jax.ShapeDtypeStruct((count, HEADS), jnp.float32),
        jax.ShapeDtypeStruct((count, HEADS), jnp.float32),
    ]
    return pl.pallas_call(
        body,
        out_shape=shapes,
        compiler_params=pltpu.CompilerParams(vmem_limit_bytes=48 * 1024 * 1024),
    )(query, keys, values, *state)


def final_kernel(q_ref, k_ref, v_ref, o1_ref, m1_ref, l1_ref, t_ref, out_ref, *, size, rows):
    width = HEADS * size
    for h in range(HEADS):
        cols = slice(h * size, (h + 1) * size)
        scores = lax.dot_general(
            q_ref[rows, cols], k_ref[:, cols], (((1,), (1,)), ((), ())),
            preferred_element_type=jnp.float32,
        )
        before = m1_ref[rows, h : h + 1]
        theirs = t_ref[:, width + h : width + h + 1]
        top = jnp.maximum(jnp.maximum(before, theirs), jnp.max(scores, axis=1, keepdims=True))
        weights = jnp.exp(scores - top)
        fade, their_fade = jnp.exp(before - top), jnp.exp(theirs - top)
        total = (
            l1_ref[rows, h : h + 1] * fade
            + t_ref[:, width + STATS + h : width + STATS + h + 1] * their_fade
            + jnp.sum(weights, axis=1, keepdims=True)
        )
        summed = (
            o1_ref[rows, cols] * fade
            + t_ref[:, cols] * their_fade
            + jnp.dot(weights.astype(jnp.bfloat16), v_ref[:, cols], preferred_element_type=jnp.float32)
        )
        out_ref[:, cols] = (summed / total).astype(out_ref.dtype)


def _whole(array):
    return pl.BlockSpec(array.shape, lambda i: (0,) * array.ndim)


def _row_specs(query, keys, start, count):
    block = start // count
    width = query.shape[1]
    rows = lambda cols: pl.BlockSpec((count, cols), lambda i: (block, 0))
    return [rows(width), _whole(keys), _whole(keys), rows(width), rows(HEADS), rows(HEADS)]


def spatial_final(query, keys, values, state, theirs, start, count):
    width = query.shape[1]
    body = lambda *refs: final_kernel(
        *refs, size=width // HEADS, rows=slice(None)
    )
    return pl.pallas_call(
        body,
        grid=(1,),
        in_specs=_row_specs(query, keys, start, count) + [_whole(theirs)],
        out_specs=pl.BlockSpec((count, width), lambda i: (0, 0)),
        out_shape=jax.ShapeDtypeStruct((count, width), jnp.bfloat16),
        compiler_params=pltpu.CompilerParams(vmem_limit_bytes=48 * 1024 * 1024),
    )(query, keys, values, *state, theirs)


def spatial_partial(query, keys, values):
    return _attention_call(partial_kernel, query, keys, values, ())


def spatial_merge(query, keys, values, state, start, count):
    width = query.shape[1]
    size = width // HEADS
    body = lambda *refs: merge_kernel(*refs, size=size, rows=slice(None))
    return pl.pallas_call(
        body,
        grid=(1,),
        in_specs=_row_specs(query, keys, start, count),
        out_specs=pl.BlockSpec((count, width + 2 * STATS), lambda i: (0, 0)),
        out_shape=jax.ShapeDtypeStruct((count, width + 2 * STATS), jnp.float32),
        compiler_params=pltpu.CompilerParams(vmem_limit_bytes=48 * 1024 * 1024),
    )(query, keys, values, *state)


def spread_y(rows):
    ring = lax.axis_size("y")
    pieces = [rows]
    for shift in sorted(range(1, ring), key=lambda s: -min(s, ring - s)):
        pairs = [(i, (i + shift) % ring) for i in range(ring)]
        pieces.append(lax.ppermute(rows, "y", pairs))
    return jnp.concatenate(pieces, axis=0)


def attend_cells(block_qkv):
    frames, cells = (block_qkv.shape[0], block_qkv.shape[1])
    width = block_qkv.shape[2] // 3
    size = width // HEADS
    scale = 1.0 / math.sqrt(size)
    query = block_qkv[:, :, :width].reshape(frames, cells, HEADS, size)
    keys = block_qkv[:, :, width : 2 * width].reshape(frames, cells, HEADS, size)
    values = block_qkv[:, :, 2 * width :].reshape(frames, cells, HEADS, size)
    del scale
    scores = jnp.einsum("fche,gche->chfg", query, keys, preferred_element_type=jnp.float32)
    later = jnp.arange(frames)[:, None] >= jnp.arange(frames)[None, :]
    scores = jnp.where(later, scores, -1e30)
    peak = jnp.max(scores, axis=3, keepdims=True)
    weights = jnp.exp(scores - peak)
    total = jnp.sum(weights, axis=3)
    summed = jnp.einsum(
        "chfg,gche->fche", weights.astype(jnp.bfloat16), values, preferred_element_type=jnp.float32
    )
    context = summed / jnp.transpose(total, (2, 0, 1))[..., None]
    return context.reshape(frames, cells, width).astype(jnp.bfloat16)


def layer(
    tokens, norm_spatial, w_spatial, w_spatial_out, norm_temporal, w_temporal, w_temporal_out
):
    frames_here, rows, width = tokens.shape
    count = frames_here * rows
    resid = tokens.reshape(count, width).astype(jnp.float32)
    normed = layer_norm(resid, norm_spatial).astype(jnp.bfloat16)
    w_query = w_spatial[:, :width] * jnp.asarray(1.0 / math.sqrt(width // HEADS), w_spatial.dtype)
    query = jnp.dot(normed, w_query, preferred_element_type=jnp.float32).astype(jnp.bfloat16)
    partner = lax.ppermute(normed, "zhi", [(0, 1), (1, 0)])
    swap = [(0, 1), (1, 0)]
    both = jnp.concatenate([lax.ppermute(query, "core", swap), query], axis=0)
    w_pairs = w_spatial[:, width:]
    near_rows = spread_y(normed)
    near = jnp.dot(near_rows, w_pairs, preferred_element_type=jnp.float32).astype(jnp.bfloat16)
    state = spatial_partial(both, near[:, :width], near[:, width:])
    far_rows = spread_y(partner)
    far = jnp.dot(far_rows, w_pairs, preferred_element_type=jnp.float32).astype(jnp.bfloat16)
    theirs = spatial_merge(both, far[:, :width], far[:, width:], state, 0, count)
    theirs = lax.ppermute(theirs, "core", swap)
    context = spatial_final(both, far[:, :width], far[:, width:], state, theirs, count, count)
    after = resid + jnp.dot(context, w_spatial_out, preferred_element_type=jnp.float32)
    second = layer_norm(after, norm_temporal).astype(jnp.bfloat16)
    owners = lax.axis_size(("x", "zlo"))
    share = rows // owners
    second = second.reshape(frames_here, owners, share, width)
    gathered = lax.all_to_all(second, ("x", "zlo"), split_axis=1, concat_axis=0, tiled=True)
    frames_all = gathered.shape[0]
    w_temporal = w_temporal.at[:, :width].multiply(
        jnp.asarray(1.0 / math.sqrt(width // HEADS), w_temporal.dtype)
    )
    qkv_t = jnp.dot(
        gathered.reshape(frames_all * share, width), w_temporal, preferred_element_type=jnp.float32
    ).astype(jnp.bfloat16)
    context_t = attend_cells(qkv_t.reshape(frames_all, share, 3 * width))
    context_t = context_t.reshape(frames_all, 1, share, width)
    returned = lax.all_to_all(context_t, ("x", "zlo"), split_axis=0, concat_axis=1, tiled=True)
    mixed = after + jnp.dot(
        returned.reshape(count, width), w_temporal_out, preferred_element_type=jnp.float32
    )
    return mixed.reshape(frames_here, rows, width).astype(jnp.bfloat16)


def solution(mesh):
    frame_n, row_n = mesh.devices.shape
    devices = mesh.devices.reshape(4, frame_n // 4, row_n // 4, 2, 2)
    fine = Mesh(devices, ("x", "zlo", "y", "zhi", "core"))
    grid_spec = P(("x", "zlo"), ("y", "zhi", "core"), None)
    in_specs = (grid_spec, P(), P(), P(), P(), P(), P())
    return jax.shard_map(layer, mesh=fine, in_specs=in_specs, out_specs=grid_spec, check_vma=False)
```

```python
import math

import jax
import jax.numpy as jnp
from jax import lax
from jax.experimental import pallas as pl
from jax.experimental.pallas import tpu as pltpu
from jax.sharding import Mesh

from jax.sharding import PartitionSpec as P

HEADS = 8
STATS = 64


def layer_norm(rows, gain):
    mean = jnp.mean(rows, axis=-1, keepdims=True)
    centred = rows - mean
    spread = jnp.mean(centred * centred, axis=-1, keepdims=True)
    return centred * lax.rsqrt(spread + 1e-05) * gain


def _scores(q_ref, k_ref, cols, scale):
    del scale
    return lax.dot_general(
        q_ref[:, cols], k_ref[:, cols], (((1,), (1,)), ((), ())),
        preferred_element_type=jnp.float32,
    )


def partial_kernel(q_ref, k_ref, v_ref, o_ref, m_ref, l_ref, *, size, scale):
    for h in range(HEADS):
        cols = slice(h * size, (h + 1) * size)
        scores = _scores(q_ref, k_ref, cols, scale)
        peak = jnp.max(scores, axis=1, keepdims=True)
        weights = jnp.exp(scores - peak)
        l_ref[:, h : h + 1] = jnp.sum(weights, axis=1, keepdims=True)
        m_ref[:, h : h + 1] = peak
        o_ref[:, cols] = jnp.dot(
            weights.astype(jnp.bfloat16), v_ref[:, cols], preferred_element_type=jnp.float32
        )


def merge_kernel(q_ref, k_ref, v_ref, o1_ref, m1_ref, l1_ref, out_ref, *, size, rows):
    width = HEADS * size
    for h in range(HEADS):
        cols = slice(h * size, (h + 1) * size)
        scores = lax.dot_general(
            q_ref[rows, cols], k_ref[:, cols], (((1,), (1,)), ((), ())),
            preferred_element_type=jnp.float32,
        )
        before = m1_ref[rows, h : h + 1]
        peak = jnp.maximum(before, jnp.max(scores, axis=1, keepdims=True))
        weights = jnp.exp(scores - peak)
        fade = jnp.exp(before - peak)
        total = l1_ref[rows, h : h + 1] * fade + jnp.sum(weights, axis=1, keepdims=True)
        out_ref[:, cols] = o1_ref[rows, cols] * fade + jnp.dot(
            weights.astype(jnp.bfloat16), v_ref[:, cols], preferred_element_type=jnp.float32
        )
        out_ref[:, width + h : width + h + 1] = peak
        out_ref[:, width + STATS + h : width + STATS + h + 1] = total


def _attention_call(kernel, query, keys, values, state):
    count, width = query.shape
    size = width // HEADS
    body = lambda *refs: kernel(*refs, size=size, scale=1.0 / math.sqrt(size))
    shapes = [
        jax.ShapeDtypeStruct((count, width), jnp.float32),
        jax.ShapeDtypeStruct((count, HEADS), jnp.float32),
        jax.ShapeDtypeStruct((count, HEADS), jnp.float32),
    ]
    return pl.pallas_call(
        body,
        out_shape=shapes,
        compiler_params=pltpu.CompilerParams(vmem_limit_bytes=48 * 1024 * 1024),
    )(query, keys, values, *state)


def final_kernel(q_ref, k_ref, v_ref, o1_ref, m1_ref, l1_ref, t_ref, out_ref, *, size, rows):
    width = HEADS * size
    for h in range(HEADS):
        cols = slice(h * size, (h + 1) * size)
        scores = lax.dot_general(
            q_ref[rows, cols], k_ref[:, cols], (((1,), (1,)), ((), ())),
            preferred_element_type=jnp.float32,
        )
        before = m1_ref[rows, h : h + 1]
        theirs = t_ref[:, width + h : width + h + 1]
        top = jnp.maximum(jnp.maximum(before, theirs), jnp.max(scores, axis=1, keepdims=True))
        weights = jnp.exp(scores - top)
        fade, their_fade = jnp.exp(before - top), jnp.exp(theirs - top)
        total = (
            l1_ref[rows, h : h + 1] * fade
            + t_ref[:, width + STATS + h : width + STATS + h + 1] * their_fade
            + jnp.sum(weights, axis=1, keepdims=True)
        )
        summed = (
            o1_ref[rows, cols] * fade
            + t_ref[:, cols] * their_fade
            + jnp.dot(weights.astype(jnp.bfloat16), v_ref[:, cols], preferred_element_type=jnp.float32)
        )
        out_ref[:, cols] = (summed / total).astype(out_ref.dtype)


def _whole(array):
    return pl.BlockSpec(array.shape, lambda i: (0,) * array.ndim)


def _row_specs(query, keys, start, count):
    block = start // count
    width = query.shape[1]
    rows = lambda cols: pl.BlockSpec((count, cols), lambda i: (block, 0))
    return [rows(width), _whole(keys), _whole(keys), rows(width), rows(HEADS), rows(HEADS)]


def spatial_final(query, keys, values, state, theirs, start, count):
    width = query.shape[1]
    body = lambda *refs: final_kernel(
        *refs, size=width // HEADS, rows=slice(None)
    )
    return pl.pallas_call(
        body,
        grid=(1,),
        in_specs=_row_specs(query, keys, start, count) + [_whole(theirs)],
        out_specs=pl.BlockSpec((count, width), lambda i: (0, 0)),
        out_shape=jax.ShapeDtypeStruct((count, width), jnp.bfloat16),
        compiler_params=pltpu.CompilerParams(vmem_limit_bytes=48 * 1024 * 1024),
    )(query, keys, values, *state, theirs)


def spatial_partial(query, keys, values):
    return _attention_call(partial_kernel, query, keys, values, ())


def spatial_merge(query, keys, values, state, start, count):
    width = query.shape[1]
    size = width // HEADS
    body = lambda *refs: merge_kernel(*refs, size=size, rows=slice(None))
    return pl.pallas_call(
        body,
        grid=(1,),
        in_specs=_row_specs(query, keys, start, count),
        out_specs=pl.BlockSpec((count, width + 2 * STATS), lambda i: (0, 0)),
        out_shape=jax.ShapeDtypeStruct((count, width + 2 * STATS), jnp.float32),
        compiler_params=pltpu.CompilerParams(vmem_limit_bytes=48 * 1024 * 1024),
    )(query, keys, values, *state)


def spread_y(rows):
    ring = lax.axis_size("y")
    pieces = [rows]
    for shift in sorted(range(1, ring), key=lambda s: -min(s, ring - s)):
        pairs = [(i, (i + shift) % ring) for i in range(ring)]
        pieces.append(lax.ppermute(rows, "y", pairs))
    return pieces


def attend_cells(block_qkv):
    cells, frames = (block_qkv.shape[0], block_qkv.shape[1])
    width = block_qkv.shape[2] // 3
    size = width // HEADS
    query = block_qkv[:, :, :width].reshape(cells, frames, HEADS, size)
    keys = block_qkv[:, :, width : 2 * width].reshape(cells, frames, HEADS, size)
    values = block_qkv[:, :, 2 * width :].reshape(cells, frames, HEADS, size)
    scores = jnp.einsum("cfhe,cghe->chfg", query, keys, preferred_element_type=jnp.float32)
    later = jnp.arange(frames)[:, None] >= jnp.arange(frames)[None, :]
    scores = jnp.where(later, scores, -1e30)
    peak = jnp.max(scores, axis=3, keepdims=True)
    weights = jnp.exp(scores - peak)
    total = jnp.sum(weights, axis=3)
    summed = jnp.einsum(
        "chfg,cghe->cfhe", weights.astype(jnp.bfloat16), values, preferred_element_type=jnp.float32
    )
    context = summed / jnp.transpose(total, (0, 2, 1))[..., None]
    return context.reshape(cells, frames, width).astype(jnp.bfloat16)


def layer(
    tokens, norm_spatial, w_spatial, w_spatial_out, norm_temporal, w_temporal, w_temporal_out
):
    frames_here, rows, width = tokens.shape
    count = frames_here * rows
    resid = tokens.reshape(count, width).astype(jnp.float32)
    normed = layer_norm(resid, norm_spatial).astype(jnp.bfloat16)
    w_query = w_spatial[:, :width] * jnp.asarray(1.0 / math.sqrt(width // HEADS), w_spatial.dtype)
    query = jnp.dot(normed, w_query, preferred_element_type=jnp.float32).astype(jnp.bfloat16)
    partner = lax.ppermute(normed, "zhi", [(0, 1), (1, 0)])
    swap = [(0, 1), (1, 0)]
    both = jnp.concatenate([lax.ppermute(query, "core", swap), query], axis=0)
    w_pairs = w_spatial[:, width:]
    near_pieces = spread_y(normed)
    far_pieces = spread_y(partner)
    near_rows = jnp.concatenate(near_pieces + [partner], axis=0)
    far_rows = jnp.concatenate(far_pieces[1:], axis=0)
    near = jnp.dot(near_rows, w_pairs, preferred_element_type=jnp.float32).astype(jnp.bfloat16)
    state = spatial_partial(both, near[:, :width], near[:, width:])
    far = jnp.dot(far_rows, w_pairs, preferred_element_type=jnp.float32).astype(jnp.bfloat16)
    theirs = spatial_merge(both, far[:, :width], far[:, width:], state, 0, count)
    theirs = lax.ppermute(theirs, "core", swap)
    context = spatial_final(both, far[:, :width], far[:, width:], state, theirs, count, count)
    after = resid + jnp.dot(context, w_spatial_out, preferred_element_type=jnp.float32)
    second = layer_norm(after, norm_temporal).astype(jnp.bfloat16)
    owners = lax.axis_size(("x", "zlo"))
    share = rows // owners
    second = second.reshape(owners, share, frames_here, width)
    gathered = lax.all_to_all(second, ("x", "zlo"), split_axis=0, concat_axis=2, tiled=True)
    frames_all = gathered.shape[2]
    w_temporal = w_temporal.at[:, :width].multiply(
        jnp.asarray(1.0 / math.sqrt(width // HEADS), w_temporal.dtype)
    )
    qkv_t = jnp.dot(
        gathered.reshape(share * frames_all, width), w_temporal, preferred_element_type=jnp.float32
    ).astype(jnp.bfloat16)
    context_t = attend_cells(qkv_t.reshape(share, frames_all, 3 * width))
    returned = lax.all_to_all(context_t, ("x", "zlo"), split_axis=1, concat_axis=0, tiled=True)
    mixed = after + jnp.dot(
        returned.reshape(count, width), w_temporal_out, preferred_element_type=jnp.float32
    )
    return mixed.reshape(frames_here, rows, width).astype(jnp.bfloat16)


def solution(mesh):
    frame_n, row_n = mesh.devices.shape
    devices = mesh.devices.reshape(4, frame_n // 4, row_n // 4, 2, 2)
    fine = Mesh(devices, ("x", "zlo", "y", "zhi", "core"))
    grid_spec = P(("x", "zlo"), ("y", "zhi", "core"), None)
    in_specs = (grid_spec, P(), P(), P(), P(), P(), P())
    return jax.shard_map(layer, mesh=fine, in_specs=in_specs, out_specs=grid_spec, check_vma=False)
```

```python
import math

import jax
import jax.numpy as jnp
from jax import lax
from jax.experimental import pallas as pl
from jax.experimental.pallas import tpu as pltpu
from jax.sharding import Mesh

from jax.sharding import PartitionSpec as P

HEADS = 8
STATS = 64


def layer_norm(rows, gain):
    mean = jnp.mean(rows, axis=-1, keepdims=True)
    centred = rows - mean
    spread = jnp.mean(centred * centred, axis=-1, keepdims=True)
    return centred * lax.rsqrt(spread + 1e-05) * gain


def _scores(q_ref, k_ref, cols, scale):
    del scale
    return lax.dot_general(
        q_ref[:, cols], k_ref[:, cols], (((1,), (1,)), ((), ())),
        preferred_element_type=jnp.float32,
    )


def partial_kernel(q_ref, k_ref, v_ref, o_ref, m_ref, l_ref, *, size, scale):
    for h in range(HEADS):
        cols = slice(h * size, (h + 1) * size)
        scores = _scores(q_ref, k_ref, cols, scale)
        peak = jnp.max(scores, axis=1, keepdims=True)
        weights = jnp.exp(scores - peak)
        l_ref[:, h : h + 1] = jnp.sum(weights, axis=1, keepdims=True)
        m_ref[:, h : h + 1] = peak
        o_ref[:, cols] = jnp.dot(
            weights.astype(jnp.bfloat16), v_ref[:, cols], preferred_element_type=jnp.float32
        )


def merge_kernel(q_ref, k_ref, v_ref, o1_ref, m1_ref, l1_ref, out_ref, *, size, rows):
    width = HEADS * size
    for h in range(HEADS):
        cols = slice(h * size, (h + 1) * size)
        scores = lax.dot_general(
            q_ref[rows, cols], k_ref[:, cols], (((1,), (1,)), ((), ())),
            preferred_element_type=jnp.float32,
        )
        before = m1_ref[rows, h : h + 1]
        peak = jnp.maximum(before, jnp.max(scores, axis=1, keepdims=True))
        weights = jnp.exp(scores - peak)
        fade = jnp.exp(before - peak)
        total = l1_ref[rows, h : h + 1] * fade + jnp.sum(weights, axis=1, keepdims=True)
        out_ref[:, cols] = o1_ref[rows, cols] * fade + jnp.dot(
            weights.astype(jnp.bfloat16), v_ref[:, cols], preferred_element_type=jnp.float32
        )
        out_ref[:, width + h : width + h + 1] = peak
        out_ref[:, width + STATS + h : width + STATS + h + 1] = total


def _attention_call(kernel, query, keys, values, state):
    count, width = query.shape
    size = width // HEADS
    body = lambda *refs: kernel(*refs, size=size, scale=1.0 / math.sqrt(size))
    shapes = [
        jax.ShapeDtypeStruct((count, width), jnp.float32),
        jax.ShapeDtypeStruct((count, HEADS), jnp.float32),
        jax.ShapeDtypeStruct((count, HEADS), jnp.float32),
    ]
    return pl.pallas_call(
        body,
        out_shape=shapes,
        compiler_params=pltpu.CompilerParams(vmem_limit_bytes=48 * 1024 * 1024),
    )(query, keys, values, *state)


def final_kernel(q_ref, k_ref, v_ref, o1_ref, m1_ref, l1_ref, t_ref, out_ref, *, size, rows):
    width = HEADS * size
    for h in range(HEADS):
        cols = slice(h * size, (h + 1) * size)
        scores = lax.dot_general(
            q_ref[rows, cols], k_ref[:, cols], (((1,), (1,)), ((), ())),
            preferred_element_type=jnp.float32,
        )
        before = m1_ref[rows, h : h + 1]
        theirs = t_ref[:, width + h : width + h + 1]
        top = jnp.maximum(jnp.maximum(before, theirs), jnp.max(scores, axis=1, keepdims=True))
        weights = jnp.exp(scores - top)
        fade, their_fade = jnp.exp(before - top), jnp.exp(theirs - top)
        total = (
            l1_ref[rows, h : h + 1] * fade
            + t_ref[:, width + STATS + h : width + STATS + h + 1] * their_fade
            + jnp.sum(weights, axis=1, keepdims=True)
        )
        summed = (
            o1_ref[rows, cols] * fade
            + t_ref[:, cols] * their_fade
            + jnp.dot(weights.astype(jnp.bfloat16), v_ref[:, cols], preferred_element_type=jnp.float32)
        )
        out_ref[:, cols] = (summed / total).astype(out_ref.dtype)


def _whole(array):
    return pl.BlockSpec(array.shape, lambda i: (0,) * array.ndim)


def _row_specs(query, keys, start, count):
    block = start // count
    width = query.shape[1]
    rows = lambda cols: pl.BlockSpec((count, cols), lambda i: (block, 0))
    return [rows(width), _whole(keys), _whole(keys), rows(width), rows(HEADS), rows(HEADS)]


def spatial_final(query, keys, values, state, theirs, start, count):
    width = query.shape[1]
    body = lambda *refs: final_kernel(
        *refs, size=width // HEADS, rows=slice(None)
    )
    return pl.pallas_call(
        body,
        grid=(1,),
        in_specs=_row_specs(query, keys, start, count) + [_whole(theirs)],
        out_specs=pl.BlockSpec((count, width), lambda i: (0, 0)),
        out_shape=jax.ShapeDtypeStruct((count, width), jnp.bfloat16),
        compiler_params=pltpu.CompilerParams(vmem_limit_bytes=48 * 1024 * 1024),
    )(query, keys, values, *state, theirs)


def spatial_partial(query, keys, values):
    return _attention_call(partial_kernel, query, keys, values, ())


def spatial_merge(query, keys, values, state, start, count):
    width = query.shape[1]
    size = width // HEADS
    body = lambda *refs: merge_kernel(*refs, size=size, rows=slice(None))
    return pl.pallas_call(
        body,
        grid=(1,),
        in_specs=_row_specs(query, keys, start, count),
        out_specs=pl.BlockSpec((count, width + 2 * STATS), lambda i: (0, 0)),
        out_shape=jax.ShapeDtypeStruct((count, width + 2 * STATS), jnp.float32),
        compiler_params=pltpu.CompilerParams(vmem_limit_bytes=48 * 1024 * 1024),
    )(query, keys, values, *state)


def spread_y(rows):
    ring = lax.axis_size("y")
    pieces = [rows]
    for shift in sorted(range(1, ring), key=lambda s: -min(s, ring - s)):
        pairs = [(i, (i + shift) % ring) for i in range(ring)]
        pieces.append(lax.ppermute(rows, "y", pairs))
    return jnp.concatenate(pieces, axis=0)


def attend_cells(block_qkv):
    cells, frames = (block_qkv.shape[0], block_qkv.shape[1])
    width = block_qkv.shape[2] // 3
    size = width // HEADS
    query = block_qkv[:, :, :width].reshape(cells, frames, HEADS, size)
    keys = block_qkv[:, :, width : 2 * width].reshape(cells, frames, HEADS, size)
    values = block_qkv[:, :, 2 * width :].reshape(cells, frames, HEADS, size)
    scores = jnp.einsum("cfhe,cghe->chfg", query, keys, preferred_element_type=jnp.float32)
    later = jnp.arange(frames)[:, None] >= jnp.arange(frames)[None, :]
    scores = jnp.where(later, scores, -1e30)
    peak = jnp.max(scores, axis=3, keepdims=True)
    weights = jnp.exp(scores - peak)
    total = jnp.sum(weights, axis=3)
    summed = jnp.einsum(
        "chfg,cghe->cfhe", weights.astype(jnp.bfloat16), values, preferred_element_type=jnp.float32
    )
    context = summed / jnp.transpose(total, (0, 2, 1))[..., None]
    return context.reshape(cells, frames, width).astype(jnp.bfloat16)


def layer(
    tokens, norm_spatial, w_spatial, w_spatial_out, norm_temporal, w_temporal, w_temporal_out
):
    frames_here, rows, width = tokens.shape
    count = frames_here * rows
    resid = tokens.reshape(count, width).astype(jnp.float32)
    normed = layer_norm(resid, norm_spatial).astype(jnp.bfloat16)
    w_query = w_spatial[:, :width] * jnp.asarray(1.0 / math.sqrt(width // HEADS), w_spatial.dtype)
    query = jnp.dot(normed, w_query, preferred_element_type=jnp.float32).astype(jnp.bfloat16)
    partner = lax.ppermute(normed, "zhi", [(0, 1), (1, 0)])
    swap = [(0, 1), (1, 0)]
    both = jnp.concatenate([lax.ppermute(query, "core", swap), query], axis=0)
    w_pairs = w_spatial[:, width:]
    near_rows = spread_y(normed)
    near = jnp.dot(near_rows, w_pairs, preferred_element_type=jnp.float32).astype(jnp.bfloat16)
    state = spatial_partial(both, near[:, :width], near[:, width:])
    far_rows = spread_y(partner)
    far = jnp.dot(far_rows, w_pairs, preferred_element_type=jnp.float32).astype(jnp.bfloat16)
    theirs = spatial_merge(both, far[:, :width], far[:, width:], state, 0, count)
    theirs = lax.ppermute(theirs, "core", swap)
    context = spatial_final(both, far[:, :width], far[:, width:], state, theirs, count, count)
    after = resid + jnp.dot(context, w_spatial_out, preferred_element_type=jnp.float32)
    second = layer_norm(after, norm_temporal).astype(jnp.bfloat16)
    owners = lax.axis_size(("x", "zlo"))
    share = rows // owners
    second = second.reshape(owners, share, frames_here, width)
    gathered = lax.all_to_all(second, ("x", "zlo"), split_axis=0, concat_axis=2, tiled=True)
    frames_all = gathered.shape[2]
    w_temporal = w_temporal.at[:, :width].multiply(
        jnp.asarray(1.0 / math.sqrt(width // HEADS), w_temporal.dtype)
    )
    qkv_t = jnp.dot(
        gathered.reshape(share * frames_all, width), w_temporal, preferred_element_type=jnp.float32
    ).astype(jnp.bfloat16)
    context_t = attend_cells(qkv_t.reshape(share, frames_all, 3 * width))
    returned = lax.all_to_all(context_t, ("x", "zlo"), split_axis=1, concat_axis=0, tiled=True)
    mixed = after + jnp.dot(
        returned.reshape(count, width), w_temporal_out, preferred_element_type=jnp.float32
    )
    return mixed.reshape(frames_here, rows, width).astype(jnp.bfloat16)


def solution(mesh):
    frame_n, row_n = mesh.devices.shape
    devices = mesh.devices.reshape(4, frame_n // 4, row_n // 4, 2, 2)
    fine = Mesh(devices, ("x", "zlo", "y", "zhi", "core"))
    grid_spec = P(("x", "zlo"), ("y", "zhi", "core"), None)
    in_specs = (grid_spec, P(), P(), P(), P(), P(), P())
    return jax.shard_map(layer, mesh=fine, in_specs=in_specs, out_specs=grid_spec, check_vma=False)
```
